768 devices in a mesh: seq: 16 (over x, y_hi), mp: 48 (over z, y_lo, core).
Axes of the slice: x: 4, y: 8 (y_hi: 4, y_lo: 2; y = y_hi * 2 + y_lo), z: 12, core: 2. Of those that a mesh axis runs over, the one named last changes fastest.
Arguments:
- queries: bfloat16 [16, 48, 1280, 256], P('seq', 'mp'), may hold values from -6 to 6
- key_rows: bfloat16 [16, 48, 1280, 128], P('seq', 'mp'), may hold values from -6 to 6
- value_rows: bfloat16 [16, 48, 1280, 128], P('seq', 'mp'), may hold values from -6 to 6
Outputs:
- attended: bfloat16 [16, 48, 1280, 256], P('seq', 'mp')
The draws below stay inside these ranges and needn't reach their ends.
All inputs are finite; a program needn't handle non-finite values.
Results may differ from the reference program's by a relative error of at most 0.0055.
Values may be sent and summed in bfloat16 or wider, within the bound.
No kernel may reach another device: no remote copies, remote signals or barrier semaphores. Data moves between devices by JAX's collectives and lax.ppermute only.
A program may use at most 64 MiB of HBM per device.

```python
import jax
import jax.numpy as jnp
from jax import lax

HD = 128
KVH = 8
QPK = 2
WINDOW = 1024
BLOCK_ROWS = 1280
SPAN_SHARDS = 16
HEAD_ROW_PAIRS = 48
N_MP = 48


def joint_draw(key):
    folded_random = jax.random.fold_in(key, 4242)
    query_random_seed, key_random_seed = jax.random.split(folded_random, 2)
    query_shape = (SPAN_SHARDS, HEAD_ROW_PAIRS, BLOCK_ROWS, QPK, HD)
    key_shape = (SPAN_SHARDS, HEAD_ROW_PAIRS, BLOCK_ROWS, HD)
    query_draw = jax.random.truncated_normal(query_random_seed, -6.0, 6.0, query_shape, jnp.float32)
    key_draw = jax.random.truncated_normal(key_random_seed, -6.0, 6.0, key_shape, jnp.float32)
    return (query_draw.reshape(SPAN_SHARDS, HEAD_ROW_PAIRS, BLOCK_ROWS, QPK * HD), key_draw)


def draw_queries(key, part):
    return joint_draw(key)[0].astype(jnp.bfloat16)


def draw_key_rows(key, part):
    return joint_draw(key)[1].astype(jnp.bfloat16)


def level_of(key, extent, shards, low, largest):
    level = 1.0
    for dim, parts in shards:
        draws = jax.random.uniform(jax.random.fold_in(jax.random.fold_in(key, 6), dim), (parts,), jnp.float32, low / len(shards), largest / len(shards))
        level = level * jnp.repeat(jnp.exp(draws), extent[dim] // parts).reshape((-1,) + (1,) * (len(extent) - 1 - dim))
    return level


def gaussian(stream_key, dims, spread, bound, shards=(), kind=jnp.bfloat16):
    values = jax.random.normal(stream_key, dims, jnp.float32) * spread
    if len(shards) > 0:
        values = level_of(stream_key, dims, shards, -0.22, 0.18) * values
    return jnp.clip(values, min=-bound, max=bound).astype(kind)


def setup_inputs(seed: int = 0) -> dict:
    key_of = jax.random.split(jax.random.key(seed), 4)
    queries = draw_queries(jax.random.fold_in(key_of[3], 71), 0)
    key_rows = draw_key_rows(jax.random.fold_in(key_of[3], 71), 0)
    value_rows = gaussian(key_of[2], (SPAN_SHARDS, HEAD_ROW_PAIRS, BLOCK_ROWS, HD), 1.0, 6.0, ((0, 16), (1, 48)))
    return dict(queries=queries, key_rows=key_rows, value_rows=value_rows)


scale_factor = 168.0 ** -0.5


def regroup(grouped_in, last_width):
    block_count = N_MP // KVH
    return grouped_in.reshape(SPAN_SHARDS * block_count, KVH, BLOCK_ROWS, last_width)


def reference(queries, key_rows, value_rows):
    block_count = N_MP // KVH
    group_count = SPAN_SHARDS * block_count
    query_all = regroup(queries, QPK * HD).reshape(group_count, KVH, BLOCK_ROWS, QPK, HD)
    key_all = regroup(key_rows, HD)
    value_all = regroup(value_rows, HD)
    key_prior = jnp.concatenate([jnp.zeros_like(key_all[:1]), key_all[:-1]], axis=0)[:, :, BLOCK_ROWS - WINDOW:]
    value_prior = jnp.concatenate([jnp.zeros_like(value_all[:1]), value_all[:-1]], axis=0)[:, :, BLOCK_ROWS - WINDOW:]
    numbers = jnp.arange(group_count, dtype=jnp.int32)
    query_pos = lax.broadcasted_iota(jnp.int32, (BLOCK_ROWS, WINDOW + BLOCK_ROWS), 0)
    key_pos = lax.broadcasted_iota(jnp.int32, (BLOCK_ROWS, WINDOW + BLOCK_ROWS), 1) - WINDOW
    base_valid = (key_pos <= query_pos) & (query_pos - key_pos < WINDOW)

    def one_block(packed):
        query_group, key_group, key_before, value_group, value_before, block_number = packed
        keys_all = jnp.concatenate([key_before, key_group], axis=1).astype(jnp.float32)
        values_all = jnp.concatenate([value_before, value_group], axis=1).astype(jnp.float32)
        scores = jnp.einsum("hrpd,hkd->hprk", query_group.astype(jnp.float32), keys_all) * scale_factor
        valid = base_valid & ((key_pos >= 0) | (block_number > 0))
        scores = jnp.where(valid, scores, -jnp.inf)
        row_top = jnp.max(scores, axis=-1, keepdims=True)
        probable = jnp.exp(scores - row_top)
        row_total = jnp.sum(probable, axis=-1, keepdims=True)
        weights = lax.optimization_barrier(probable.astype(jnp.bfloat16)).astype(jnp.float32)
        context = jnp.einsum("hprk,hkd->hprd", weights, values_all) / row_total
        context = jnp.transpose(context, (0, 2, 1, 3)).astype(jnp.bfloat16)
        return context.reshape(KVH, BLOCK_ROWS, QPK * HD)

    result = lax.map(one_block, (query_all, key_all, key_prior, value_all, value_prior, numbers))
    return result.reshape(SPAN_SHARDS, block_count * KVH, BLOCK_ROWS, QPK * HD)
```

```python
import functools

import jax
import jax.numpy as jnp
from jax import lax
from jax.experimental import pallas as pl
from jax.experimental.pallas import tpu as pltpu
from jax.sharding import PartitionSpec as P

KVH = 8
QPK = 2
WINDOW = 1024
QUERY_TILE = 256
LANES = 128


scale_factor = 168.0 ** (-0.5)


def tile_scores(query_tile, key_tile):
    raw = lax.dot_general(
        query_tile, key_tile, (((1,), (1,)), ((), ())), preferred_element_type=jnp.float32
    )
    return raw * scale_factor


def local_kernel(q_ref, k_ref, v_ref, out_ref, top_ref, total_ref, acc_ref):
    row_count = q_ref.shape[0]
    halo_rows = top_ref.shape[0]
    for first_row in range(0, row_count, QUERY_TILE):
        low_key = max(0, first_row - WINDOW + 1) // LANES * LANES
        high_key = first_row + QUERY_TILE
        scores = tile_scores(q_ref[first_row:high_key, :], k_ref[low_key:high_key, :])
        query_pos = first_row + lax.broadcasted_iota(jnp.int32, scores.shape, 0)
        key_pos = low_key + lax.broadcasted_iota(jnp.int32, scores.shape, 1)
        valid = (key_pos <= query_pos) & (query_pos - key_pos < WINDOW)
        scores = jnp.where(valid, scores, -jnp.inf)
        row_top = jnp.max(scores, axis=1, keepdims=True)
        probable = jnp.exp(scores - row_top)
        row_total = jnp.sum(probable, axis=1, keepdims=True)
        context = jnp.dot(
            probable.astype(jnp.bfloat16),
            v_ref[low_key:high_key, :],
            preferred_element_type=jnp.float32,
        )
        if first_row < halo_rows:
            top_ref[first_row:high_key, :] = jnp.broadcast_to(row_top, (QUERY_TILE, LANES))
            total_ref[first_row:high_key, :] = jnp.broadcast_to(row_total, (QUERY_TILE, LANES))
            acc_ref[first_row:high_key, :] = context
        else:
            out_ref[first_row:high_key, :] = (context / row_total).astype(out_ref.dtype)


def halo_kernel(opening_ref, q_ref, halo_ref, top_ref, total_ref, acc_ref, partial_ref, out_ref):
    halo_rows = top_ref.shape[0]
    window = halo_ref.shape[1]
    out_ref[halo_rows:, :] = partial_ref[halo_rows:, :]
    shut = opening_ref[0] != 0
    for first_row in range(0, halo_rows, QUERY_TILE):
        high_row = first_row + QUERY_TILE
        scores = tile_scores(q_ref[first_row:high_row, :], halo_ref[0, first_row:window, :])
        query_pos = first_row + lax.broadcasted_iota(jnp.int32, scores.shape, 0)
        key_pos = first_row + lax.broadcasted_iota(jnp.int32, scores.shape, 1)
        valid = (key_pos > query_pos) & jnp.logical_not(shut)
        scores = jnp.where(valid, scores, -jnp.inf)
        local_top = top_ref[first_row:high_row, 0:1]
        row_top = jnp.maximum(local_top, jnp.max(scores, axis=1, keepdims=True))
        probable = jnp.exp(scores - row_top)
        halo_total = jnp.sum(probable, axis=1, keepdims=True)
        halo_context = jnp.dot(
            probable.astype(jnp.bfloat16),
            halo_ref[1, first_row:window, :],
            preferred_element_type=jnp.float32,
        )
        rescale = jnp.exp(local_top - row_top)
        context = rescale * acc_ref[first_row:high_row, :] + halo_context
        row_total = rescale * total_ref[first_row:high_row, 0:1] + halo_total
        out_ref[first_row:high_row, :] = (context / row_total).astype(out_ref.dtype)


def local_part(query_local, key_local, value_local, halo_rows):
    row_count, width = query_local.shape
    head_size = key_local.shape[1]
    heads = width // head_size
    head_block = pl.BlockSpec((row_count, head_size), lambda p: (0, p))
    whole = pl.BlockSpec((row_count, head_size), lambda p: (0, 0))
    stat_block = pl.BlockSpec((None, halo_rows, LANES), lambda p: (p, 0, 0))
    acc_block = pl.BlockSpec((None, halo_rows, head_size), lambda p: (p, 0, 0))
    flops = 4 * heads * row_count * (WINDOW + QUERY_TILE) * head_size
    return pl.pallas_call(
        local_kernel,
        grid=(heads,),
        in_specs=[head_block, whole, whole],
        out_specs=[head_block, stat_block, stat_block, acc_block],
        out_shape=[
            jax.ShapeDtypeStruct((row_count, width), query_local.dtype),
            jax.ShapeDtypeStruct((heads, halo_rows, LANES), jnp.float32),
            jax.ShapeDtypeStruct((heads, halo_rows, LANES), jnp.float32),
            jax.ShapeDtypeStruct((heads, halo_rows, head_size), jnp.float32),
        ],
        cost_estimate=pl.CostEstimate(
            flops=flops,
            transcendentals=heads * row_count * (WINDOW + QUERY_TILE),
            bytes_accessed=4 * row_count * width + 12 * heads * halo_rows * LANES,
        ),
    )(query_local, key_local, value_local)


def halo_part(opening, query_local, halo, top, total, acc, partial_out):
    row_count, width = query_local.shape
    head_size = halo.shape[2]
    window = halo.shape[1]
    heads = width // head_size
    halo_rows = top.shape[1]
    query_block = pl.BlockSpec((row_count, head_size), lambda p, o: (0, p))
    halo_block = pl.BlockSpec((2, window, head_size), lambda p, o: (0, 0, 0))
    stat_block = pl.BlockSpec((None, halo_rows, LANES), lambda p, o: (p, 0, 0))
    acc_block = pl.BlockSpec((None, halo_rows, head_size), lambda p, o: (p, 0, 0))
    flops = 4 * heads * halo_rows * window * head_size
    return pl.pallas_call(
        halo_kernel,
        grid_spec=pltpu.PrefetchScalarGridSpec(
            num_scalar_prefetch=1,
            grid=(heads,),
            in_specs=[
                query_block,
                halo_block,
                stat_block,
                stat_block,
                acc_block,
                query_block,
            ],
            out_specs=query_block,
        ),
        out_shape=jax.ShapeDtypeStruct((row_count, width), partial_out.dtype),
        input_output_aliases={6: 0},
        cost_estimate=pl.CostEstimate(
            flops=flops,
            transcendentals=heads * halo_rows * window,
            bytes_accessed=3 * row_count * width * 2 + 12 * heads * halo_rows * LANES,
        ),
    )(opening, query_local, halo, top, total, acc, partial_out)


def per_device(queries, key_rows, value_rows):
    row_count = queries.shape[2]
    seq_count = lax.axis_size("seq")
    model_count = lax.axis_size("mp")
    blocks = model_count // KVH
    row_block = lax.axis_index("mp") // KVH
    opening = jnp.logical_and(lax.axis_index("seq") == 0, row_block == 0)
    opening = opening.astype(jnp.int32).reshape(1)
    query_local = queries[0, 0]
    key_local = key_rows[0, 0]
    value_local = value_rows[0, 0]
    halo_source = jnp.stack([key_local[row_count - WINDOW :], value_local[row_count - WINDOW :]])
    route = []
    for s in range(seq_count):
        for m in range(model_count):
            if m >= KVH:
                route.append((s * model_count + m - KVH, s * model_count + m))
            elif s > 0:
                route.append(((s - 1) * model_count + (blocks - 1) * KVH + m, s * model_count + m))
    halo = lax.ppermute(halo_source, ("seq", "mp"), route)
    halo_rows = -(-(WINDOW - 1) // QUERY_TILE) * QUERY_TILE
    partial_out, top, total, acc = local_part(query_local, key_local, value_local, halo_rows)
    attended = halo_part(opening, query_local, halo, top, total, acc, partial_out)
    return attended.reshape(1, 1, row_count, queries.shape[3])


def solution(mesh):
    in_specs = (P("seq", "mp", None, None), P("seq", "mp", None, None), P("seq", "mp", None, None))
    out_specs = P("seq", "mp", None, None)
    return jax.shard_map(
        per_device, mesh=mesh, in_specs=in_specs, out_specs=out_specs, check_vma=False
    )
```

```python
import jax
import jax.numpy as jnp
from jax import lax
from jax.experimental import pallas as pl
from jax.experimental.pallas import tpu as pltpu
from jax.sharding import PartitionSpec as P

KVH = 8
QPK = 2
WINDOW = 1024
QUERY_TILE = 256
LANES = 128


scale_factor = 168.0 ** (-0.5)


def tile_scores(query_tile, key_tile):
    raw = lax.dot_general(
        query_tile, key_tile, (((1,), (1,)), ((), ())), preferred_element_type=jnp.float32
    )
    return raw * scale_factor


def packed_stats(row_top, row_total):
    lane = lax.broadcasted_iota(jnp.int32, (row_top.shape[0], LANES), 1)
    return jnp.where(lane < LANES // 2, row_top, row_total)


def local_kernel(q_ref, k_ref, v_ref, out_ref, stats_ref, acc_ref):
    row_count = q_ref.shape[0]
    halo_rows = stats_ref.shape[0]
    for first_row in range(0, row_count, QUERY_TILE):
        low_key = max(0, first_row - WINDOW + 1) // LANES * LANES
        high_key = first_row + QUERY_TILE
        scores = tile_scores(q_ref[first_row:high_key, :], k_ref[low_key:high_key, :])
        query_pos = first_row + lax.broadcasted_iota(jnp.int32, scores.shape, 0)
        key_pos = low_key + lax.broadcasted_iota(jnp.int32, scores.shape, 1)
        valid = (key_pos <= query_pos) & (query_pos - key_pos < WINDOW)
        scores = jnp.where(valid, scores, -jnp.inf)
        row_top = jnp.max(scores, axis=1, keepdims=True)
        probable = jnp.exp(scores - row_top)
        row_total = jnp.sum(probable, axis=1, keepdims=True)
        context = jnp.dot(
            probable.astype(jnp.bfloat16),
            v_ref[low_key:high_key, :],
            preferred_element_type=jnp.float32,
        )
        if first_row < halo_rows:
            stats_ref[first_row:high_key, :] = packed_stats(row_top, row_total)
            acc_ref[first_row:high_key, :] = context
        else:
            out_ref[first_row:high_key, :] = (context / row_total).astype(out_ref.dtype)


def halo_tile(first_row, shut, q_ref, halo_ref, stats_ref, acc_ref, out_ref):
    window = halo_ref.shape[1]
    query_tile = q_ref[...]
    near_row = first_row + QUERY_TILE
    near = tile_scores(query_tile, halo_ref[0, first_row:near_row, :])
    above = lax.broadcasted_iota(jnp.int32, near.shape, 1) > lax.broadcasted_iota(
        jnp.int32, near.shape, 0
    )
    near = jnp.where(above, near, -jnp.inf)
    parts = [(near, halo_ref[1, first_row:near_row, :])]
    if near_row < window:
        far = tile_scores(query_tile, halo_ref[0, near_row:window, :])
        parts.append((far, halo_ref[1, near_row:window, :]))
    local_top = stats_ref[:, 0:1]
    local_total = stats_ref[:, LANES // 2 : LANES // 2 + 1]
    local_context = acc_ref[...]
    row_top = local_top
    for scores, _ in parts:
        row_top = jnp.maximum(row_top, jnp.max(scores, axis=1, keepdims=True))
    rescale = jnp.exp(local_top - row_top)
    context = rescale * local_context
    row_total = rescale * local_total
    for scores, values in parts:
        probable = jnp.exp(scores - row_top)
        row_total = row_total + jnp.sum(probable, axis=1, keepdims=True)
        context = context + jnp.dot(
            probable.astype(jnp.bfloat16), values, preferred_element_type=jnp.float32
        )
    joined = context / row_total
    alone = local_context / local_total
    out_ref[...] = jnp.where(shut, alone, joined).astype(out_ref.dtype)


def halo_kernel(opening_ref, q_ref, halo_ref, stats_ref, acc_ref, _, out_ref):
    tile = pl.program_id(1)
    shut = opening_ref[0] != 0
    for index in range(pl.num_programs(1)):

        @pl.when(tile == index)
        def _():
            halo_tile(index * QUERY_TILE, shut, q_ref, halo_ref, stats_ref, acc_ref, out_ref)


def local_part(query_local, key_local, value_local, halo_rows):
    row_count, width = query_local.shape
    head_size = key_local.shape[1]
    heads = width // head_size
    head_block = pl.BlockSpec((row_count, head_size), lambda p: (0, p))
    whole = pl.BlockSpec((row_count, head_size), lambda p: (0, 0))
    stat_block = pl.BlockSpec((None, halo_rows, LANES), lambda p: (p, 0, 0))
    acc_block = pl.BlockSpec((None, halo_rows, head_size), lambda p: (p, 0, 0))
    flops = 4 * heads * row_count * (WINDOW + QUERY_TILE) * head_size
    return pl.pallas_call(
        local_kernel,
        grid=(heads,),
        in_specs=[head_block, whole, whole],
        out_specs=[head_block, stat_block, acc_block],
        out_shape=[
            jax.ShapeDtypeStruct((row_count, width), query_local.dtype),
            jax.ShapeDtypeStruct((heads, halo_rows, LANES), jnp.float32),
            jax.ShapeDtypeStruct((heads, halo_rows, head_size), jnp.float32),
        ],
        cost_estimate=pl.CostEstimate(
            flops=flops,
            transcendentals=heads * row_count * (WINDOW + QUERY_TILE),
            bytes_accessed=4 * row_count * width + 8 * heads * halo_rows * LANES,
        ),
    )(query_local, key_local, value_local)


def halo_part(opening, query_local, halo, stats, acc, partial_out):
    row_count, width = query_local.shape
    head_size = halo.shape[2]
    window = halo.shape[1]
    heads = width // head_size
    halo_rows = stats.shape[1]
    tiles = halo_rows // QUERY_TILE
    query_block = pl.BlockSpec((QUERY_TILE, head_size), lambda p, i, o: (i, p))
    stat_block = pl.BlockSpec((None, QUERY_TILE, LANES), lambda p, i, o: (p, i, 0))
    acc_block = pl.BlockSpec((None, QUERY_TILE, head_size), lambda p, i, o: (p, i, 0))
    flops = 2 * heads * halo_rows * window * head_size
    return pl.pallas_call(
        halo_kernel,
        grid_spec=pltpu.PrefetchScalarGridSpec(
            num_scalar_prefetch=1,
            grid=(heads, tiles),
            in_specs=[
                query_block,
                pl.BlockSpec(memory_space=pltpu.VMEM),
                stat_block,
                acc_block,
                pl.BlockSpec(memory_space=pl.ANY),
            ],
            out_specs=query_block,
        ),
        out_shape=jax.ShapeDtypeStruct((row_count, width), partial_out.dtype),
        input_output_aliases={5: 0},
        cost_estimate=pl.CostEstimate(
            flops=flops,
            transcendentals=heads * halo_rows * window // 2,
            bytes_accessed=2 * halo_rows * width * 2 + 8 * heads * halo_rows * LANES,
        ),
    )(opening, query_local, halo, stats, acc, partial_out)


def per_device(queries, key_rows, value_rows):
    row_count = queries.shape[2]
    seq_count = lax.axis_size("seq")
    model_count = lax.axis_size("mp")
    blocks = model_count // KVH
    row_block = lax.axis_index("mp") // KVH
    opening = jnp.logical_and(lax.axis_index("seq") == 0, row_block == 0)
    opening = opening.astype(jnp.int32).reshape(1)
    query_local = queries[0, 0]
    key_local = key_rows[0, 0]
    value_local = value_rows[0, 0]
    halo_source = jnp.stack([key_local[row_count - WINDOW :], value_local[row_count - WINDOW :]])
    route = []
    for s in range(seq_count):
        for m in range(model_count):
            if m >= KVH:
                route.append((s * model_count + m - KVH, s * model_count + m))
            elif s > 0:
                route.append(((s - 1) * model_count + (blocks - 1) * KVH + m, s * model_count + m))
    halo = lax.ppermute(halo_source, ("seq", "mp"), route)
    halo_rows = -(-(WINDOW - 1) // QUERY_TILE) * QUERY_TILE
    partial_out, stats, acc = local_part(query_local, key_local, value_local, halo_rows)
    attended = halo_part(opening, query_local, halo, stats, acc, partial_out)
    return attended.reshape(1, 1, row_count, queries.shape[3])


def solution(mesh):
    in_specs = (P("seq", "mp", None, None), P("seq", "mp", None, None), P("seq", "mp", None, None))
    out_specs = P("seq", "mp", None, None)
    return jax.shard_map(
        per_device, mesh=mesh, in_specs=in_specs, out_specs=out_specs, check_vma=False
    )
```

```python
import jax
import jax.numpy as jnp
from jax import lax
from jax.experimental import pallas as pl
from jax.experimental.pallas import tpu as pltpu
from jax.sharding import PartitionSpec as P

KVH = 8
QPK = 2
WINDOW = 1024
QUERY_TILE = 256
LANES = 128


scale_factor = 168.0 ** (-0.5)


def tile_scores(query_tile, key_tile):
    raw = lax.dot_general(
        query_tile, key_tile, (((1,), (1,)), ((), ())), preferred_element_type=jnp.float32
    )
    return raw * scale_factor


def packed_stats(row_top, row_total):
    lane = lax.broadcasted_iota(jnp.int32, (row_top.shape[0], LANES), 1)
    return jnp.where(lane < LANES // 2, row_top, row_total)


def local_kernel(q_ref, k_ref, v_ref, out_ref, stats_ref, acc_ref):
    row_count = q_ref.shape[0]
    halo_rows = stats_ref.shape[0]
    for first_row in range(0, row_count, QUERY_TILE):
        low_key = max(0, first_row - WINDOW + 1) // LANES * LANES
        high_key = first_row + QUERY_TILE
        scores = tile_scores(q_ref[first_row:high_key, :], k_ref[low_key:high_key, :])
        query_pos = first_row + lax.broadcasted_iota(jnp.int32, scores.shape, 0)
        key_pos = low_key + lax.broadcasted_iota(jnp.int32, scores.shape, 1)
        valid = (key_pos <= query_pos) & (query_pos - key_pos < WINDOW)
        scores = jnp.where(valid, scores, -jnp.inf)
        row_top = jnp.max(scores, axis=1, keepdims=True)
        probable = jnp.exp(scores - row_top)
        row_total = jnp.sum(probable, axis=1, keepdims=True)
        context = jnp.dot(
            probable.astype(jnp.bfloat16),
            v_ref[low_key:high_key, :],
            preferred_element_type=jnp.float32,
        )
        if first_row < halo_rows:
            stats_ref[first_row:high_key, :] = packed_stats(row_top, row_total)
            acc_ref[first_row:high_key, :] = context
        else:
            out_ref[first_row:high_key, :] = (context / row_total).astype(out_ref.dtype)


def merge_tile(query_tile, chunk_ref, offset, first_row, low_key, high_key, local):
    parts = []
    far_key = low_key
    if first_row >= low_key:
        near_row = first_row + QUERY_TILE
        near = tile_scores(query_tile, chunk_ref[0, first_row - offset : near_row - offset, :])
        above = lax.broadcasted_iota(jnp.int32, near.shape, 1) > lax.broadcasted_iota(
            jnp.int32, near.shape, 0
        )
        near = jnp.where(above, near, -jnp.inf)
        parts.append((near, chunk_ref[1, first_row - offset : near_row - offset, :]))
        far_key = near_row
    if far_key < high_key:
        far = tile_scores(query_tile, chunk_ref[0, far_key - offset : high_key - offset, :])
        parts.append((far, chunk_ref[1, far_key - offset : high_key - offset, :]))
    local_top, local_total, local_context = local
    row_top = local_top
    for scores, _ in parts:
        row_top = jnp.maximum(row_top, jnp.max(scores, axis=1, keepdims=True))
    rescale = jnp.exp(local_top - row_top)
    context = rescale * local_context
    row_total = rescale * local_total
    for scores, values in parts:
        probable = jnp.exp(scores - row_top)
        row_total = row_total + jnp.sum(probable, axis=1, keepdims=True)
        context = context + jnp.dot(
            probable.astype(jnp.bfloat16), values, preferred_element_type=jnp.float32
        )
    return row_top, row_total, context


def read_stats(stats_ref, acc_ref, first_row):
    high_row = first_row + QUERY_TILE
    return (
        stats_ref[first_row:high_row, 0:1],
        stats_ref[first_row:high_row, LANES // 2 : LANES // 2 + 1],
        acc_ref[first_row:high_row, :],
    )


def finish(shut, local, merged):
    joined = merged[2] / merged[1]
    alone = local[2] / local[1]
    return jnp.where(shut, alone, joined)


def far_kernel(
    opening_ref, q_ref, chunk_ref, stats_ref, acc_ref, partial_ref, out_ref, open_stats, open_acc
):
    halo_rows = stats_ref.shape[0]
    offset = halo_rows - chunk_ref.shape[1]
    shut = opening_ref[0] != 0
    out_ref[halo_rows:, :] = partial_ref[halo_rows:, :]
    for first_row in range(0, halo_rows, QUERY_TILE):
        high_row = first_row + QUERY_TILE
        local = read_stats(stats_ref, acc_ref, first_row)
        merged = merge_tile(
            q_ref[first_row:high_row, :], chunk_ref, offset, first_row, max(first_row, offset),
            halo_rows, local,
        )
        if first_row >= offset:
            out_ref[first_row:high_row, :] = finish(shut, local, merged).astype(out_ref.dtype)
        else:
            kept = [jnp.where(shut, a, b) for a, b in zip(local, merged)]
            open_stats[first_row:high_row, :] = packed_stats(kept[0], kept[1])
            open_acc[first_row:high_row, :] = kept[2]


def near_kernel(opening_ref, q_ref, chunk_ref, stats_ref, acc_ref, _, out_ref):
    open_rows = stats_ref.shape[0]
    shut = opening_ref[0] != 0
    for first_row in range(0, open_rows, QUERY_TILE):
        high_row = first_row + QUERY_TILE
        local = read_stats(stats_ref, acc_ref, first_row)
        merged = merge_tile(
            q_ref[first_row:high_row, :], chunk_ref, 0, first_row, first_row, open_rows, local
        )
        out_ref[first_row:high_row, :] = finish(shut, local, merged).astype(out_ref.dtype)


def local_part(query_local, key_local, value_local, halo_rows):
    row_count, width = query_local.shape
    head_size = key_local.shape[1]
    heads = width // head_size
    head_block = pl.BlockSpec((row_count, head_size), lambda p: (0, p))
    whole = pl.BlockSpec((row_count, head_size), lambda p: (0, 0))
    stat_block = pl.BlockSpec((None, halo_rows, LANES), lambda p: (p, 0, 0))
    acc_block = pl.BlockSpec((None, halo_rows, head_size), lambda p: (p, 0, 0))
    flops = 4 * heads * row_count * (WINDOW + QUERY_TILE) * head_size
    return pl.pallas_call(
        local_kernel,
        grid=(heads,),
        in_specs=[head_block, whole, whole],
        out_specs=[head_block, stat_block, acc_block],
        out_shape=[
            jax.ShapeDtypeStruct((row_count, width), query_local.dtype),
            jax.ShapeDtypeStruct((heads, halo_rows, LANES), jnp.float32),
            jax.ShapeDtypeStruct((heads, halo_rows, head_size), jnp.float32),
        ],
        cost_estimate=pl.CostEstimate(
            flops=flops,
            transcendentals=heads * row_count * (WINDOW + QUERY_TILE),
            bytes_accessed=4 * row_count * width + 8 * heads * halo_rows * LANES,
        ),
    )(query_local, key_local, value_local)


def far_part(opening, query_local, chunk, stats, acc, partial_out):
    row_count, width = query_local.shape
    head_size = chunk.shape[2]
    chunk_rows = chunk.shape[1]
    heads = width // head_size
    halo_rows = stats.shape[1]
    open_rows = halo_rows - chunk_rows
    column = pl.BlockSpec((row_count, head_size), lambda p, o: (0, p))
    chunk_block = pl.BlockSpec(chunk.shape, lambda p, o: (0, 0, 0))
    stat_block = pl.BlockSpec((None, halo_rows, LANES), lambda p, o: (p, 0, 0))
    acc_block = pl.BlockSpec((None, halo_rows, head_size), lambda p, o: (p, 0, 0))
    open_stat_block = pl.BlockSpec((None, open_rows, LANES), lambda p, o: (p, 0, 0))
    open_acc_block = pl.BlockSpec((None, open_rows, head_size), lambda p, o: (p, 0, 0))
    flops = 2 * heads * halo_rows * chunk_rows * head_size
    return pl.pallas_call(
        far_kernel,
        grid_spec=pltpu.PrefetchScalarGridSpec(
            num_scalar_prefetch=1,
            grid=(heads,),
            in_specs=[column, chunk_block, stat_block, acc_block, column],
            out_specs=[column, open_stat_block, open_acc_block],
        ),
        out_shape=[
            jax.ShapeDtypeStruct((row_count, width), partial_out.dtype),
            jax.ShapeDtypeStruct((heads, open_rows, LANES), jnp.float32),
            jax.ShapeDtypeStruct((heads, open_rows, head_size), jnp.float32),
        ],
        input_output_aliases={5: 0},
        cost_estimate=pl.CostEstimate(
            flops=flops,
            transcendentals=heads * halo_rows * chunk_rows // 2,
            bytes_accessed=3 * row_count * width * 2 + 8 * heads * halo_rows * LANES,
        ),
    )(opening, query_local, chunk, stats, acc, partial_out)


def near_part(opening, query_local, chunk, stats, acc, partial_out):
    row_count, width = query_local.shape
    head_size = chunk.shape[2]
    heads = width // head_size
    open_rows = stats.shape[1]
    query_block = pl.BlockSpec((open_rows, head_size), lambda p, o: (0, p))
    chunk_block = pl.BlockSpec(chunk.shape, lambda p, o: (0, 0, 0))
    stat_block = pl.BlockSpec((None, open_rows, LANES), lambda p, o: (p, 0, 0))
    acc_block = pl.BlockSpec((None, open_rows, head_size), lambda p, o: (p, 0, 0))
    flops = 2 * heads * open_rows * open_rows * head_size
    return pl.pallas_call(
        near_kernel,
        grid_spec=pltpu.PrefetchScalarGridSpec(
            num_scalar_prefetch=1,
            grid=(heads,),
            in_specs=[
                query_block,
                chunk_block,
                stat_block,
                acc_block,
                pl.BlockSpec(memory_space=pl.ANY),
            ],
            out_specs=query_block,
        ),
        out_shape=jax.ShapeDtypeStruct((row_count, width), partial_out.dtype),
        input_output_aliases={5: 0},
        cost_estimate=pl.CostEstimate(
            flops=flops,
            transcendentals=heads * open_rows * open_rows,
            bytes_accessed=2 * open_rows * width * 2 + 8 * heads * open_rows * LANES,
        ),
    )(opening, query_local, chunk, stats, acc, partial_out)


def per_device(queries, key_rows, value_rows):
    row_count = queries.shape[2]
    seq_count = lax.axis_size("seq")
    model_count = lax.axis_size("mp")
    blocks = model_count // KVH
    row_block = lax.axis_index("mp") // KVH
    opening = jnp.logical_and(lax.axis_index("seq") == 0, row_block == 0)
    opening = opening.astype(jnp.int32).reshape(1)
    query_local = queries[0, 0]
    key_local = key_rows[0, 0]
    value_local = value_rows[0, 0]
    split_row = row_count - WINDOW + QUERY_TILE
    far_source = jnp.stack([key_local[split_row:], value_local[split_row:]])
    near_source = jnp.stack(
        [key_local[row_count - WINDOW : split_row], value_local[row_count - WINDOW : split_row]]
    )
    route = []
    for s in range(seq_count):
        for m in range(model_count):
            if m >= KVH:
                route.append((s * model_count + m - KVH, s * model_count + m))
            elif s > 0:
                route.append(((s - 1) * model_count + (blocks - 1) * KVH + m, s * model_count + m))
    far_chunk = lax.ppermute(far_source, ("seq", "mp"), route)
    near_chunk = lax.ppermute(near_source, ("seq", "mp"), route)
    halo_rows = WINDOW
    partial_out, stats, acc = local_part(query_local, key_local, value_local, halo_rows)
    partial_out, open_stats, open_acc = far_part(
        opening, query_local, far_chunk, stats, acc, partial_out
    )
    attended = near_part(opening, query_local, near_chunk, open_stats, open_acc, partial_out)
    return attended.reshape(1, 1, row_count, queries.shape[3])


def solution(mesh):
    in_specs = (P("seq", "mp", None, None), P("seq", "mp", None, None), P("seq", "mp", None, None))
    out_specs = P("seq", "mp", None, None)
    return jax.shard_map(
        per_device, mesh=mesh, in_specs=in_specs, out_specs=out_specs, check_vma=False
    )
```

```python
import jax
import jax.numpy as jnp
from jax import lax
from jax.experimental import pallas as pl
from jax.experimental.pallas import tpu as pltpu
from jax.sharding import PartitionSpec as P

KVH = 8
QPK = 2
WINDOW = 1024
QUERY_TILE = 256
HALO_TILE = 128
LANES = 128


scale_factor = 168.0 ** (-0.5)


def tile_scores(query_tile, key_tile):
    raw = lax.dot_general(
        query_tile, key_tile, (((1,), (1,)), ((), ())), preferred_element_type=jnp.float32
    )
    return raw * scale_factor


def packed_stats(row_top, row_total):
    lane = lax.broadcasted_iota(jnp.int32, (row_top.shape[0], LANES), 1)
    return jnp.where(lane < LANES // 2, row_top, row_total)


def local_kernel(q_ref, k_ref, v_ref, out_ref, stats_ref, acc_ref):
    row_count = q_ref.shape[0]
    halo_rows = stats_ref.shape[0]
    for first_row in range(0, row_count, QUERY_TILE):
        low_key = max(0, first_row - WINDOW + 1) // LANES * LANES
        high_key = first_row + QUERY_TILE
        scores = tile_scores(q_ref[first_row:high_key, :], k_ref[low_key:high_key, :])
        query_pos = first_row + lax.broadcasted_iota(jnp.int32, scores.shape, 0)
        key_pos = low_key + lax.broadcasted_iota(jnp.int32, scores.shape, 1)
        valid = (key_pos <= query_pos) & (query_pos - key_pos < WINDOW)
        scores = jnp.where(valid, scores, -jnp.inf)
        row_top = jnp.max(scores, axis=1, keepdims=True)
        probable = jnp.exp(scores - row_top)
        row_total = jnp.sum(probable, axis=1, keepdims=True)
        context = jnp.dot(
            probable.astype(jnp.bfloat16),
            v_ref[low_key:high_key, :],
            preferred_element_type=jnp.float32,
        )
        if first_row < halo_rows:
            stats_ref[first_row:high_key, :] = packed_stats(row_top, row_total)
            acc_ref[first_row:high_key, :] = context
        else:
            out_ref[first_row:high_key, :] = (context / row_total).astype(out_ref.dtype)


def merge_tile(query_tile, key_ref, value_ref, first_row, low_key, high_key, local):
    parts = []
    far_key = low_key
    if first_row >= low_key:
        near_row = first_row + query_tile.shape[0]
        near = tile_scores(query_tile, key_ref[first_row:near_row, :])
        above = lax.broadcasted_iota(jnp.int32, near.shape, 1) > lax.broadcasted_iota(
            jnp.int32, near.shape, 0
        )
        near = jnp.where(above, near, -jnp.inf)
        parts.append((near, value_ref[first_row:near_row, :]))
        far_key = near_row
    if far_key < high_key:
        far = tile_scores(query_tile, key_ref[far_key:high_key, :])
        parts.append((far, value_ref[far_key:high_key, :]))
    local_top, local_total, local_context = local
    row_top = local_top
    for scores, _ in parts:
        row_top = jnp.maximum(row_top, jnp.max(scores, axis=1, keepdims=True))
    rescale = jnp.exp(local_top - row_top)
    context = rescale * local_context
    row_total = rescale * local_total
    for scores, values in parts:
        probable = jnp.exp(scores - row_top)
        row_total = row_total + jnp.sum(probable, axis=1, keepdims=True)
        context = context + jnp.dot(
            probable.astype(jnp.bfloat16), values, preferred_element_type=jnp.float32
        )
    return row_top, row_total, context


def read_stats(stats_ref, acc_ref, first_row, rows):
    high_row = first_row + rows
    return (
        stats_ref[first_row:high_row, 0:1],
        stats_ref[first_row:high_row, LANES // 2 : LANES // 2 + 1],
        acc_ref[first_row:high_row, :],
    )


def finish(shut, local, merged):
    joined = merged[2] / merged[1]
    alone = local[2] / local[1]
    return jnp.where(shut, alone, joined)


def halo_kernel(opening_ref, q_ref, key_ref, value_ref, stats_ref, acc_ref, partial_ref, out_ref):
    halo_rows = stats_ref.shape[0]
    shut = opening_ref[0] != 0
    out_ref[halo_rows:, :] = partial_ref[halo_rows:, :]
    for first_row in range(0, halo_rows, HALO_TILE):
        high_row = first_row + HALO_TILE
        local = read_stats(stats_ref, acc_ref, first_row, HALO_TILE)
        merged = merge_tile(
            q_ref[first_row:high_row, :], key_ref, value_ref, first_row, first_row, halo_rows,
            local,
        )
        out_ref[first_row:high_row, :] = finish(shut, local, merged).astype(out_ref.dtype)


def local_part(query_local, key_local, value_local, halo_rows):
    row_count, width = query_local.shape
    head_size = key_local.shape[1]
    heads = width // head_size
    head_block = pl.BlockSpec((row_count, head_size), lambda p: (0, p))
    whole = pl.BlockSpec((row_count, head_size), lambda p: (0, 0))
    stat_block = pl.BlockSpec((None, halo_rows, LANES), lambda p: (p, 0, 0))
    acc_block = pl.BlockSpec((None, halo_rows, head_size), lambda p: (p, 0, 0))
    flops = 4 * heads * row_count * (WINDOW + QUERY_TILE) * head_size
    return pl.pallas_call(
        local_kernel,
        grid=(heads,),
        in_specs=[head_block, whole, whole],
        out_specs=[head_block, stat_block, acc_block],
        out_shape=[
            jax.ShapeDtypeStruct((row_count, width), query_local.dtype),
            jax.ShapeDtypeStruct((heads, halo_rows, LANES), jnp.float32),
            jax.ShapeDtypeStruct((heads, halo_rows, head_size), jnp.float32),
        ],
        cost_estimate=pl.CostEstimate(
            flops=flops,
            transcendentals=heads * row_count * (WINDOW + QUERY_TILE),
            bytes_accessed=4 * row_count * width + 8 * heads * halo_rows * LANES,
        ),
    )(query_local, key_local, value_local)


def halo_part(opening, query_local, halo_keys, halo_values, stats, acc, partial_out):
    row_count, width = query_local.shape
    window, head_size = halo_keys.shape
    heads = width // head_size
    halo_rows = stats.shape[1]
    column = pl.BlockSpec((row_count, head_size), lambda p, o: (0, p))
    halo_block = pl.BlockSpec((window, head_size), lambda p, o: (0, 0))
    stat_block = pl.BlockSpec((None, halo_rows, LANES), lambda p, o: (p, 0, 0))
    acc_block = pl.BlockSpec((None, halo_rows, head_size), lambda p, o: (p, 0, 0))
    flops = 2 * heads * halo_rows * window * head_size
    return pl.pallas_call(
        halo_kernel,
        grid_spec=pltpu.PrefetchScalarGridSpec(
            num_scalar_prefetch=1,
            grid=(heads,),
            in_specs=[column, halo_block, halo_block, stat_block, acc_block, column],
            out_specs=column,
        ),
        out_shape=jax.ShapeDtypeStruct((row_count, width), partial_out.dtype),
        input_output_aliases={6: 0},
        cost_estimate=pl.CostEstimate(
            flops=flops,
            transcendentals=heads * halo_rows * window // 2,
            bytes_accessed=3 * row_count * width * 2 + 8 * heads * halo_rows * LANES,
        ),
    )(opening, query_local, halo_keys, halo_values, stats, acc, partial_out)


def per_device(queries, key_rows, value_rows):
    row_count = queries.shape[2]
    seq_count = lax.axis_size("seq")
    model_count = lax.axis_size("mp")
    blocks = model_count // KVH
    row_block = lax.axis_index("mp") // KVH
    opening = jnp.logical_and(lax.axis_index("seq") == 0, row_block == 0)
    opening = opening.astype(jnp.int32).reshape(1)
    query_local = queries[0, 0]
    key_local = key_rows[0, 0]
    value_local = value_rows[0, 0]
    route = []
    for s in range(seq_count):
        for m in range(model_count):
            if m >= KVH:
                route.append((s * model_count + m - KVH, s * model_count + m))
            elif s > 0:
                route.append(((s - 1) * model_count + (blocks - 1) * KVH + m, s * model_count + m))
    halo_keys = lax.ppermute(key_local[row_count - WINDOW :], ("seq", "mp"), route)
    halo_values = lax.ppermute(value_local[row_count - WINDOW :], ("seq", "mp"), route)
    halo_rows = WINDOW
    partial_out, stats, acc = local_part(query_local, key_local, value_local, halo_rows)
    attended = halo_part(opening, query_local, halo_keys, halo_values, stats, acc, partial_out)
    return attended.reshape(1, 1, row_count, queries.shape[3])


def solution(mesh):
    in_specs = (P("seq", "mp", None, None), P("seq", "mp", None, None), P("seq", "mp", None, None))
    out_specs = P("seq", "mp", None, None)
    return jax.shard_map(
        per_device, mesh=mesh, in_specs=in_specs, out_specs=out_specs, check_vma=False
    )
```

```python
import jax
import jax.numpy as jnp
from jax import lax
from jax.experimental import pallas as pl
from jax.experimental.pallas import tpu as pltpu
from jax.sharding import PartitionSpec as P

KVH = 8
QPK = 2
WINDOW = 1024
QUERY_TILE = 256
LANES = 128


scale_factor = 168.0 ** (-0.5)


def tile_scores(query_tile, key_tile):
    raw = lax.dot_general(
        query_tile, key_tile, (((1,), (1,)), ((), ())), preferred_element_type=jnp.float32
    )
    return raw * scale_factor


def packed_stats(row_top, row_total):
    lane = lax.broadcasted_iota(jnp.int32, (row_top.shape[0], LANES), 1)
    return jnp.where(lane < LANES // 2, row_top, row_total)


def local_kernel(q_ref, k_ref, v_ref, out_ref, stats_ref, acc_ref):
    row_count = q_ref.shape[0]
    halo_rows = stats_ref.shape[0]
    for first_row in range(0, row_count, QUERY_TILE):
        low_key = max(0, first_row - WINDOW + 1) // LANES * LANES
        high_key = first_row + QUERY_TILE
        scores = tile_scores(q_ref[first_row:high_key, :], k_ref[low_key:high_key, :])
        query_pos = first_row + lax.broadcasted_iota(jnp.int32, scores.shape, 0)
        key_pos = low_key + lax.broadcasted_iota(jnp.int32, scores.shape, 1)
        valid = (key_pos <= query_pos) & (query_pos - key_pos < WINDOW)
        scores = jnp.where(valid, scores, -jnp.inf)
        row_top = jnp.max(scores, axis=1, keepdims=True)
        probable = jnp.exp(scores - row_top)
        row_total = jnp.sum(probable, axis=1, keepdims=True)
        context = jnp.dot(
            probable.astype(jnp.bfloat16),
            v_ref[low_key:high_key, :],
            preferred_element_type=jnp.float32,
        )
        if first_row < halo_rows:
            stats_ref[first_row:high_key, :] = packed_stats(row_top, row_total)
            acc_ref[first_row:high_key, :] = context
        else:
            out_ref[first_row:high_key, :] = (context / row_total).astype(out_ref.dtype)


def read_stats(stats_ref, acc_ref, first_row, rows):
    high_row = first_row + rows
    return (
        stats_ref[first_row:high_row, 0:1],
        stats_ref[first_row:high_row, LANES // 2 : LANES // 2 + 1],
        acc_ref[first_row:high_row, :],
    )


def weigh_kernel(opening_ref, q_ref, key_ref, stats_ref, weight_ref, merged_ref):
    halo_rows = stats_ref.shape[0]
    window = key_ref.shape[0]
    shut = opening_ref[0] != 0
    column = 0
    for first_row in range(0, halo_rows, QUERY_TILE):
        high_row = first_row + QUERY_TILE
        local_top, local_total, _ = read_stats(stats_ref, stats_ref, first_row, QUERY_TILE)
        query_tile = q_ref[first_row:high_row, :]
        near = tile_scores(query_tile, key_ref[first_row:high_row, :])
        above = lax.broadcasted_iota(jnp.int32, near.shape, 1) > lax.broadcasted_iota(
            jnp.int32, near.shape, 0
        )
        parts = [jnp.where(above, near, -jnp.inf)]
        if high_row < window:
            parts.append(tile_scores(query_tile, key_ref[high_row:window, :]))
        row_top = local_top
        for scores in parts:
            row_top = jnp.maximum(row_top, jnp.max(scores, axis=1, keepdims=True))
        rescale = jnp.exp(local_top - row_top)
        row_total = rescale * local_total
        for scores in parts:
            probable = jnp.exp(scores - row_top)
            row_total = row_total + jnp.sum(probable, axis=1, keepdims=True)
            width = scores.shape[1]
            weight_ref[:, column : column + width] = probable.astype(weight_ref.dtype)
            column += width
        rescale = jnp.where(shut, 1.0, rescale)
        row_total = jnp.where(shut, local_total, row_total)
        merged_ref[first_row:high_row, :] = packed_stats(rescale, row_total)


def gather_kernel(opening_ref, weight_ref, value_ref, merged_ref, acc_ref, partial_ref, out_ref):
    halo_rows = merged_ref.shape[0]
    window = value_ref.shape[0]
    shut = opening_ref[0] != 0
    out_ref[halo_rows:, :] = partial_ref[halo_rows:, :]
    column = 0
    for first_row in range(0, halo_rows, QUERY_TILE):
        high_row = first_row + QUERY_TILE
        rescale, row_total, local_context = read_stats(merged_ref, acc_ref, first_row, QUERY_TILE)
        width = window - first_row
        context = jnp.dot(
            weight_ref[:, column : column + width],
            value_ref[first_row:window, :],
            preferred_element_type=jnp.float32,
        )
        column += width
        context = rescale * local_context + jnp.where(shut, 0.0, context)
        out_ref[first_row:high_row, :] = (context / row_total).astype(out_ref.dtype)


def local_part(query_local, key_local, value_local, halo_rows):
    row_count, width = query_local.shape
    head_size = key_local.shape[1]
    heads = width // head_size
    head_block = pl.BlockSpec((row_count, head_size), lambda p: (0, p))
    whole = pl.BlockSpec((row_count, head_size), lambda p: (0, 0))
    stat_block = pl.BlockSpec((None, halo_rows, LANES), lambda p: (p, 0, 0))
    acc_block = pl.BlockSpec((None, halo_rows, head_size), lambda p: (p, 0, 0))
    flops = 4 * heads * row_count * (WINDOW + QUERY_TILE) * head_size
    return pl.pallas_call(
        local_kernel,
        grid=(heads,),
        in_specs=[head_block, whole, whole],
        out_specs=[head_block, stat_block, acc_block],
        out_shape=[
            jax.ShapeDtypeStruct((row_count, width), query_local.dtype),
            jax.ShapeDtypeStruct((heads, halo_rows, LANES), jnp.float32),
            jax.ShapeDtypeStruct((heads, halo_rows, head_size), jnp.float32),
        ],
        cost_estimate=pl.CostEstimate(
            flops=flops,
            transcendentals=heads * row_count * (WINDOW + QUERY_TILE),
            bytes_accessed=4 * row_count * width + 8 * heads * halo_rows * LANES,
        ),
    )(query_local, key_local, value_local)


def packed_width(halo_rows, window):
    return sum(window - first_row for first_row in range(0, halo_rows, QUERY_TILE))


def weigh_part(opening, query_local, halo_keys, stats):
    row_count, width = query_local.shape
    window, head_size = halo_keys.shape
    heads = width // head_size
    halo_rows = stats.shape[1]
    weight_width = packed_width(halo_rows, window)
    column = pl.BlockSpec((row_count, head_size), lambda p, o: (0, p))
    halo_block = pl.BlockSpec((window, head_size), lambda p, o: (0, 0))
    stat_block = pl.BlockSpec((None, halo_rows, LANES), lambda p, o: (p, 0, 0))
    weight_block = pl.BlockSpec((None, QUERY_TILE, weight_width), lambda p, o: (p, 0, 0))
    return pl.pallas_call(
        weigh_kernel,
        grid_spec=pltpu.PrefetchScalarGridSpec(
            num_scalar_prefetch=1,
            grid=(heads,),
            in_specs=[column, halo_block, stat_block],
            out_specs=[weight_block, stat_block],
        ),
        out_shape=[
            jax.ShapeDtypeStruct((heads, QUERY_TILE, weight_width), jnp.bfloat16),
            jax.ShapeDtypeStruct((heads, halo_rows, LANES), jnp.float32),
        ],
        cost_estimate=pl.CostEstimate(
            flops=2 * heads * QUERY_TILE * weight_width * head_size,
            transcendentals=heads * QUERY_TILE * weight_width,
            bytes_accessed=row_count * width * 2 + 2 * heads * QUERY_TILE * weight_width
            + 8 * heads * halo_rows * LANES,
        ),
    )(opening, query_local, halo_keys, stats)


def gather_part(opening, weights, halo_values, merged, acc, partial_out):
    row_count, width = partial_out.shape
    window, head_size = halo_values.shape
    heads = width // head_size
    halo_rows = merged.shape[1]
    weight_width = weights.shape[2]
    column = pl.BlockSpec((row_count, head_size), lambda p, o: (0, p))
    halo_block = pl.BlockSpec((window, head_size), lambda p, o: (0, 0))
    stat_block = pl.BlockSpec((None, halo_rows, LANES), lambda p, o: (p, 0, 0))
    acc_block = pl.BlockSpec((None, halo_rows, head_size), lambda p, o: (p, 0, 0))
    weight_block = pl.BlockSpec((None, QUERY_TILE, weight_width), lambda p, o: (p, 0, 0))
    return pl.pallas_call(
        gather_kernel,
        grid_spec=pltpu.PrefetchScalarGridSpec(
            num_scalar_prefetch=1,
            grid=(heads,),
            in_specs=[weight_block, halo_block, stat_block, acc_block, column],
            out_specs=column,
        ),
        out_shape=jax.ShapeDtypeStruct((row_count, width), partial_out.dtype),
        input_output_aliases={5: 0},
        cost_estimate=pl.CostEstimate(
            flops=2 * heads * QUERY_TILE * weight_width * head_size,
            transcendentals=0,
            bytes_accessed=2 * heads * QUERY_TILE * weight_width + 2 * row_count * width * 2
            + 8 * heads * halo_rows * LANES,
        ),
    )(opening, weights, halo_values, merged, acc, partial_out)


def per_device(queries, key_rows, value_rows):
    row_count = queries.shape[2]
    seq_count = lax.axis_size("seq")
    model_count = lax.axis_size("mp")
    blocks = model_count // KVH
    row_block = lax.axis_index("mp") // KVH
    opening = jnp.logical_and(lax.axis_index("seq") == 0, row_block == 0)
    opening = opening.astype(jnp.int32).reshape(1)
    query_local = queries[0, 0]
    key_local = key_rows[0, 0]
    value_local = value_rows[0, 0]
    route = []
    for s in range(seq_count):
        for m in range(model_count):
            if m >= KVH:
                route.append((s * model_count + m - KVH, s * model_count + m))
            elif s > 0:
                route.append(((s - 1) * model_count + (blocks - 1) * KVH + m, s * model_count + m))
    halo_keys = lax.ppermute(key_local[row_count - WINDOW :], ("seq", "mp"), route)
    halo_values = lax.ppermute(value_local[row_count - WINDOW :], ("seq", "mp"), route)
    halo_rows = WINDOW
    partial_out, stats, acc = local_part(query_local, key_local, value_local, halo_rows)
    weights, merged = weigh_part(opening, query_local, halo_keys, stats)
    attended = gather_part(opening, weights, halo_values, merged, acc, partial_out)
    return attended.reshape(1, 1, row_count, queries.shape[3])


def solution(mesh):
    in_specs = (P("seq", "mp", None, None), P("seq", "mp", None, None), P("seq", "mp", None, None))
    out_specs = P("seq", "mp", None, None)
    return jax.shard_map(
        per_device, mesh=mesh, in_specs=in_specs, out_specs=out_specs, check_vma=False
    )
```

```python
import jax
import jax.numpy as jnp
from jax import lax
from jax.experimental import pallas as pl
from jax.experimental.pallas import tpu as pltpu
from jax.sharding import PartitionSpec as P

KVH = 8
QPK = 2
WINDOW = 1024
QUERY_TILE = 256
LANES = 128


scale_factor = 168.0 ** (-0.5)


def tile_scores(query_tile, key_tile):
    raw = lax.dot_general(
        query_tile, key_tile, (((1,), (1,)), ((), ())), preferred_element_type=jnp.float32
    )
    return raw * scale_factor


def packed_stats(row_top, row_total):
    lane = lax.broadcasted_iota(jnp.int32, (row_top.shape[0], LANES), 1)
    return jnp.where(lane < LANES // 2, row_top, row_total)


def local_kernel(q_ref, k_ref, v_ref, out_ref, stats_ref, acc_ref):
    row_count = q_ref.shape[0]
    halo_rows = stats_ref.shape[0]
    for first_row in range(0, row_count, QUERY_TILE):
        low_key = max(0, first_row - WINDOW + 1) // LANES * LANES
        high_key = first_row + QUERY_TILE
        scores = tile_scores(q_ref[first_row:high_key, :], k_ref[low_key:high_key, :])
        query_pos = first_row + lax.broadcasted_iota(jnp.int32, scores.shape, 0)
        key_pos = low_key + lax.broadcasted_iota(jnp.int32, scores.shape, 1)
        valid = (key_pos <= query_pos) & (query_pos - key_pos < WINDOW)
        scores = jnp.where(valid, scores, -jnp.inf)
        row_top = jnp.max(scores, axis=1, keepdims=True)
        probable = jnp.exp(scores - row_top)
        row_total = jnp.sum(probable, axis=1, keepdims=True)
        context = jnp.dot(
            probable.astype(jnp.bfloat16),
            v_ref[low_key:high_key, :],
            preferred_element_type=jnp.float32,
        )
        if first_row < halo_rows:
            stats_ref[first_row:high_key, :] = packed_stats(row_top, row_total)
            acc_ref[first_row:high_key, :] = context
        else:
            out_ref[first_row:high_key, :] = (context / row_total).astype(out_ref.dtype)


def read_stats(stats_ref, acc_ref, first_row, rows):
    high_row = first_row + rows
    return (
        stats_ref[first_row:high_row, 0:1],
        stats_ref[first_row:high_row, LANES // 2 : LANES // 2 + 1],
        acc_ref[first_row:high_row, :],
    )


def weigh_kernel(opening_ref, q_ref, key_ref, stats_ref, weight_ref, merged_ref):
    halo_rows = stats_ref.shape[0]
    window = key_ref.shape[0]
    shut = opening_ref[0] != 0
    column = 0
    for first_row in range(0, halo_rows, QUERY_TILE):
        high_row = first_row + QUERY_TILE
        local_top, local_total, _ = read_stats(stats_ref, stats_ref, first_row, QUERY_TILE)
        query_tile = q_ref[first_row:high_row, :]
        near = tile_scores(query_tile, key_ref[first_row:high_row, :])
        above = lax.broadcasted_iota(jnp.int32, near.shape, 1) > lax.broadcasted_iota(
            jnp.int32, near.shape, 0
        )
        parts = [jnp.where(above, near, -jnp.inf)]
        if high_row < window:
            parts.append(tile_scores(query_tile, key_ref[high_row:window, :]))
        row_top = local_top
        for scores in parts:
            row_top = jnp.maximum(row_top, jnp.max(scores, axis=1, keepdims=True))
        rescale = jnp.exp(local_top - row_top)
        row_total = rescale * local_total
        for scores in parts:
            probable = jnp.exp(scores - row_top)
            row_total = row_total + jnp.sum(probable, axis=1, keepdims=True)
            width = scores.shape[1]
            weight_ref[:, column : column + width] = probable.astype(weight_ref.dtype)
            column += width
        rescale = jnp.where(shut, 1.0, rescale)
        row_total = jnp.where(shut, local_total, row_total)
        merged_ref[first_row:high_row, :] = packed_stats(rescale, row_total)


def gather_kernel(opening_ref, weight_ref, value_ref, merged_ref, acc_ref, _, out_ref):
    halo_rows = merged_ref.shape[0]
    window = value_ref.shape[0]
    shut = opening_ref[0] != 0
    column = 0
    for first_row in range(0, halo_rows, QUERY_TILE):
        high_row = first_row + QUERY_TILE
        rescale, row_total, local_context = read_stats(merged_ref, acc_ref, first_row, QUERY_TILE)
        width = window - first_row
        context = jnp.dot(
            weight_ref[:, column : column + width],
            value_ref[first_row:window, :],
            preferred_element_type=jnp.float32,
        )
        column += width
        context = rescale * local_context + jnp.where(shut, 0.0, context)
        out_ref[first_row:high_row, :] = (context / row_total).astype(out_ref.dtype)


def local_part(query_local, key_local, value_local, halo_rows):
    row_count, width = query_local.shape
    head_size = key_local.shape[1]
    heads = width // head_size
    head_block = pl.BlockSpec((row_count, head_size), lambda p: (0, p))
    whole = pl.BlockSpec((row_count, head_size), lambda p: (0, 0))
    stat_block = pl.BlockSpec((None, halo_rows, LANES), lambda p: (p, 0, 0))
    acc_block = pl.BlockSpec((None, halo_rows, head_size), lambda p: (p, 0, 0))
    flops = 4 * heads * row_count * (WINDOW + QUERY_TILE) * head_size
    return pl.pallas_call(
        local_kernel,
        grid=(heads,),
        in_specs=[head_block, whole, whole],
        out_specs=[head_block, stat_block, acc_block],
        out_shape=[
            jax.ShapeDtypeStruct((row_count, width), query_local.dtype),
            jax.ShapeDtypeStruct((heads, halo_rows, LANES), jnp.float32),
            jax.ShapeDtypeStruct((heads, halo_rows, head_size), jnp.float32),
        ],
        cost_estimate=pl.CostEstimate(
            flops=flops,
            transcendentals=heads * row_count * (WINDOW + QUERY_TILE),
            bytes_accessed=4 * row_count * width + 8 * heads * halo_rows * LANES,
        ),
    )(query_local, key_local, value_local)


def packed_width(halo_rows, window):
    return sum(window - first_row for first_row in range(0, halo_rows, QUERY_TILE))


def weigh_part(opening, query_local, halo_keys, stats):
    row_count, width = query_local.shape
    window, head_size = halo_keys.shape
    heads = width // head_size
    halo_rows = stats.shape[1]
    weight_width = packed_width(halo_rows, window)
    column = pl.BlockSpec((row_count, head_size), lambda p, o: (0, p))
    halo_block = pl.BlockSpec((window, head_size), lambda p, o: (0, 0))
    stat_block = pl.BlockSpec((None, halo_rows, LANES), lambda p, o: (p, 0, 0))
    weight_block = pl.BlockSpec((None, QUERY_TILE, weight_width), lambda p, o: (p, 0, 0))
    return pl.pallas_call(
        weigh_kernel,
        grid_spec=pltpu.PrefetchScalarGridSpec(
            num_scalar_prefetch=1,
            grid=(heads,),
            in_specs=[column, halo_block, stat_block],
            out_specs=[weight_block, stat_block],
        ),
        out_shape=[
            jax.ShapeDtypeStruct((heads, QUERY_TILE, weight_width), jnp.bfloat16),
            jax.ShapeDtypeStruct((heads, halo_rows, LANES), jnp.float32),
        ],
        cost_estimate=pl.CostEstimate(
            flops=2 * heads * QUERY_TILE * weight_width * head_size,
            transcendentals=heads * QUERY_TILE * weight_width,
            bytes_accessed=row_count * width * 2 + 2 * heads * QUERY_TILE * weight_width
            + 8 * heads * halo_rows * LANES,
        ),
    )(opening, query_local, halo_keys, stats)


def gather_part(opening, weights, halo_values, merged, acc, partial_out):
    row_count, width = partial_out.shape
    window, head_size = halo_values.shape
    heads = width // head_size
    halo_rows = merged.shape[1]
    weight_width = weights.shape[2]
    column = pl.BlockSpec((halo_rows, head_size), lambda p, o: (0, p))
    halo_block = pl.BlockSpec((window, head_size), lambda p, o: (0, 0))
    stat_block = pl.BlockSpec((None, halo_rows, LANES), lambda p, o: (p, 0, 0))
    acc_block = pl.BlockSpec((None, halo_rows, head_size), lambda p, o: (p, 0, 0))
    weight_block = pl.BlockSpec((None, QUERY_TILE, weight_width), lambda p, o: (p, 0, 0))
    return pl.pallas_call(
        gather_kernel,
        grid_spec=pltpu.PrefetchScalarGridSpec(
            num_scalar_prefetch=1,
            grid=(heads,),
            in_specs=[
                weight_block,
                halo_block,
                stat_block,
                acc_block,
                pl.BlockSpec(memory_space=pl.ANY),
            ],
            out_specs=column,
        ),
        out_shape=jax.ShapeDtypeStruct((row_count, width), partial_out.dtype),
        input_output_aliases={5: 0},
        cost_estimate=pl.CostEstimate(
            flops=2 * heads * QUERY_TILE * weight_width * head_size,
            transcendentals=0,
            bytes_accessed=2 * heads * QUERY_TILE * weight_width + 2 * row_count * width * 2
            + 8 * heads * halo_rows * LANES,
        ),
    )(opening, weights, halo_values, merged, acc, partial_out)


def per_device(queries, key_rows, value_rows):
    row_count = queries.shape[2]
    seq_count = lax.axis_size("seq")
    model_count = lax.axis_size("mp")
    blocks = model_count // KVH
    row_block = lax.axis_index("mp") // KVH
    opening = jnp.logical_and(lax.axis_index("seq") == 0, row_block == 0)
    opening = opening.astype(jnp.int32).reshape(1)
    query_local = queries[0, 0]
    key_local = key_rows[0, 0]
    value_local = value_rows[0, 0]
    route = []
    for s in range(seq_count):
        for m in range(model_count):
            if m >= KVH:
                route.append((s * model_count + m - KVH, s * model_count + m))
            elif s > 0:
                route.append(((s - 1) * model_count + (blocks - 1) * KVH + m, s * model_count + m))
    key_tail, value_tail = lax.optimization_barrier(
        (key_local[row_count - WINDOW :], value_local[row_count - WINDOW :])
    )
    halo_keys = lax.ppermute(key_tail, ("seq", "mp"), route)
    halo_values = lax.ppermute(value_tail, ("seq", "mp"), route)
    halo_rows = WINDOW
    partial_out, stats, acc = local_part(query_local, key_local, value_local, halo_rows)
    weights, merged = weigh_part(opening, query_local, halo_keys, stats)
    attended = gather_part(opening, weights, halo_values, merged, acc, partial_out)
    return attended.reshape(1, 1, row_count, queries.shape[3])


def solution(mesh):
    in_specs = (P("seq", "mp", None, None), P("seq", "mp", None, None), P("seq", "mp", None, None))
    out_specs = P("seq", "mp", None, None)
    return jax.shard_map(
        per_device, mesh=mesh, in_specs=in_specs, out_specs=out_specs, check_vma=False
    )
```

```python
import jax
import jax.numpy as jnp
from jax import lax
from jax.experimental import pallas as pl
from jax.experimental.pallas import tpu as pltpu
from jax.sharding import PartitionSpec as P

KVH = 8
QPK = 2
WINDOW = 1024
QUERY_TILE = 256
LANES = 128


scale_factor = 168.0 ** (-0.5)


def tile_scores(query_tile, key_tile):
    raw = lax.dot_general(
        query_tile, key_tile, (((1,), (1,)), ((), ())), preferred_element_type=jnp.float32
    )
    return raw * scale_factor


def packed_stats(row_top, row_total):
    lane = lax.broadcasted_iota(jnp.int32, (row_top.shape[0], LANES), 1)
    return jnp.where(lane < LANES // 2, row_top, row_total)


def local_kernel(q_ref, k_ref, v_ref, out_ref, stats_ref, acc_ref):
    row_count = q_ref.shape[0]
    halo_rows = stats_ref.shape[0]
    for first_row in range(0, row_count, QUERY_TILE):
        low_key = max(0, first_row - WINDOW + 1) // LANES * LANES
        high_key = first_row + QUERY_TILE
        scores = tile_scores(q_ref[first_row:high_key, :], k_ref[low_key:high_key, :])
        query_pos = first_row + lax.broadcasted_iota(jnp.int32, scores.shape, 0)
        key_pos = low_key + lax.broadcasted_iota(jnp.int32, scores.shape, 1)
        valid = (key_pos <= query_pos) & (query_pos - key_pos < WINDOW)
        scores = jnp.where(valid, scores, -jnp.inf)
        row_top = jnp.max(scores, axis=1, keepdims=True)
        probable = jnp.exp(scores - row_top)
        row_total = jnp.sum(probable, axis=1, keepdims=True)
        context = jnp.dot(
            probable.astype(jnp.bfloat16),
            v_ref[low_key:high_key, :],
            preferred_element_type=jnp.float32,
        )
        if first_row < halo_rows:
            stats_ref[first_row:high_key, :] = packed_stats(row_top, row_total)
            acc_ref[first_row:high_key, :] = context
        else:
            out_ref[first_row:high_key, :] = (context / row_total).astype(out_ref.dtype)


def read_stats(stats_ref, acc_ref, first_row, rows):
    high_row = first_row + rows
    return (
        stats_ref[first_row:high_row, 0:1],
        stats_ref[first_row:high_row, LANES // 2 : LANES // 2 + 1],
        acc_ref[first_row:high_row, :],
    )


def weigh_kernel(opening_ref, q_ref, key_ref, stats_ref, weight_ref, merged_ref):
    halo_rows = stats_ref.shape[0]
    window = key_ref.shape[0]
    shut = opening_ref[0] != 0
    column = 0
    for first_row in range(0, halo_rows, QUERY_TILE):
        high_row = first_row + QUERY_TILE
        local_top, local_total, _ = read_stats(stats_ref, stats_ref, first_row, QUERY_TILE)
        query_tile = q_ref[first_row:high_row, :]
        near = tile_scores(query_tile, key_ref[first_row:high_row, :])
        above = lax.broadcasted_iota(jnp.int32, near.shape, 1) > lax.broadcasted_iota(
            jnp.int32, near.shape, 0
        )
        parts = [jnp.where(above, near, -jnp.inf)]
        if high_row < window:
            parts.append(tile_scores(query_tile, key_ref[high_row:window, :]))
        row_top = local_top
        for scores in parts:
            row_top = jnp.maximum(row_top, jnp.max(scores, axis=1, keepdims=True))
        rescale = jnp.exp(local_top - row_top)
        row_total = rescale * local_total
        for scores in parts:
            probable = jnp.exp(scores - row_top)
            row_total = row_total + jnp.sum(probable, axis=1, keepdims=True)
            width = scores.shape[1]
            weight_ref[:, column : column + width] = probable.astype(weight_ref.dtype)
            column += width
        rescale = jnp.where(shut, 1.0, rescale)
        row_total = jnp.where(shut, local_total, row_total)
        merged_ref[first_row:high_row, :] = packed_stats(rescale, row_total)


def gather_kernel(opening_ref, weight_ref, value_ref, merged_ref, acc_ref, _, out_ref):
    halo_rows = merged_ref.shape[0]
    window = value_ref.shape[0]
    shut = opening_ref[0] != 0
    column = 0
    for first_row in range(0, halo_rows, QUERY_TILE):
        high_row = first_row + QUERY_TILE
        rescale, row_total, local_context = read_stats(merged_ref, acc_ref, first_row, QUERY_TILE)
        width = window - first_row
        context = jnp.dot(
            weight_ref[:, column : column + width],
            value_ref[first_row:window, :],
            preferred_element_type=jnp.float32,
        )
        column += width
        context = rescale * local_context + jnp.where(shut, 0.0, context)
        out_ref[first_row:high_row, :] = (context / row_total).astype(out_ref.dtype)


def local_part(query_local, key_local, value_local, halo_rows):
    row_count, width = query_local.shape
    head_size = key_local.shape[1]
    heads = width // head_size
    head_block = pl.BlockSpec((row_count, head_size), lambda p: (0, p))
    whole = pl.BlockSpec((row_count, head_size), lambda p: (0, 0))
    stat_block = pl.BlockSpec((None, halo_rows, LANES), lambda p: (p, 0, 0))
    acc_block = pl.BlockSpec((None, halo_rows, head_size), lambda p: (p, 0, 0))
    flops = 4 * heads * row_count * (WINDOW + QUERY_TILE) * head_size
    return pl.pallas_call(
        local_kernel,
        grid=(heads,),
        in_specs=[head_block, whole, whole],
        out_specs=[head_block, stat_block, acc_block],
        out_shape=[
            jax.ShapeDtypeStruct((row_count, width), query_local.dtype),
            jax.ShapeDtypeStruct((heads, halo_rows, LANES), jnp.float32),
            jax.ShapeDtypeStruct((heads, halo_rows, head_size), jnp.float32),
        ],
        cost_estimate=pl.CostEstimate(
            flops=flops,
            transcendentals=heads * row_count * (WINDOW + QUERY_TILE),
            bytes_accessed=4 * row_count * width + 8 * heads * halo_rows * LANES,
        ),
    )(query_local, key_local, value_local)


def packed_width(halo_rows, window):
    return sum(window - first_row for first_row in range(0, halo_rows, QUERY_TILE))


def weigh_part(opening, query_local, halo_keys, stats):
    row_count, width = query_local.shape
    window, head_size = halo_keys.shape
    heads = width // head_size
    halo_rows = stats.shape[1]
    weight_width = packed_width(halo_rows, window)
    column = pl.BlockSpec((row_count, head_size), lambda p, o: (0, p))
    halo_block = pl.BlockSpec((window, head_size), lambda p, o: (0, 0))
    stat_block = pl.BlockSpec((None, halo_rows, LANES), lambda p, o: (p, 0, 0))
    weight_block = pl.BlockSpec((None, QUERY_TILE, weight_width), lambda p, o: (p, 0, 0))
    return pl.pallas_call(
        weigh_kernel,
        grid_spec=pltpu.PrefetchScalarGridSpec(
            num_scalar_prefetch=1,
            grid=(heads,),
            in_specs=[column, halo_block, stat_block],
            out_specs=[weight_block, stat_block],
        ),
        out_shape=[
            jax.ShapeDtypeStruct((heads, QUERY_TILE, weight_width), jnp.bfloat16),
            jax.ShapeDtypeStruct((heads, halo_rows, LANES), jnp.float32),
        ],
        cost_estimate=pl.CostEstimate(
            flops=2 * heads * QUERY_TILE * weight_width * head_size,
            transcendentals=heads * QUERY_TILE * weight_width,
            bytes_accessed=row_count * width * 2 + 2 * heads * QUERY_TILE * weight_width
            + 8 * heads * halo_rows * LANES,
        ),
    )(opening, query_local, halo_keys, stats)


def gather_part(opening, weights, halo_values, merged, acc, partial_out):
    row_count, width = partial_out.shape
    window, head_size = halo_values.shape
    heads = width // head_size
    halo_rows = merged.shape[1]
    weight_width = weights.shape[2]
    column = pl.BlockSpec((halo_rows, head_size), lambda p, o: (0, p))
    halo_block = pl.BlockSpec((window, head_size), lambda p, o: (0, 0))
    stat_block = pl.BlockSpec((None, halo_rows, LANES), lambda p, o: (p, 0, 0))
    acc_block = pl.BlockSpec((None, halo_rows, head_size), lambda p, o: (p, 0, 0))
    weight_block = pl.BlockSpec((None, QUERY_TILE, weight_width), lambda p, o: (p, 0, 0))
    return pl.pallas_call(
        gather_kernel,
        grid_spec=pltpu.PrefetchScalarGridSpec(
            num_scalar_prefetch=1,
            grid=(heads,),
            in_specs=[
                weight_block,
                halo_block,
                stat_block,
                acc_block,
                pl.BlockSpec(memory_space=pl.ANY),
            ],
            out_specs=column,
        ),
        out_shape=jax.ShapeDtypeStruct((row_count, width), partial_out.dtype),
        input_output_aliases={5: 0},
        cost_estimate=pl.CostEstimate(
            flops=2 * heads * QUERY_TILE * weight_width * head_size,
            transcendentals=0,
            bytes_accessed=2 * heads * QUERY_TILE * weight_width + 2 * row_count * width * 2
            + 8 * heads * halo_rows * LANES,
        ),
    )(opening, weights, halo_values, merged, acc, partial_out)


def per_device(queries, key_rows, value_rows):
    row_count = queries.shape[2]
    seq_count = lax.axis_size("seq")
    model_count = lax.axis_size("mp")
    blocks = model_count // KVH
    row_block = lax.axis_index("mp") // KVH
    opening = jnp.logical_and(lax.axis_index("seq") == 0, row_block == 0)
    opening = opening.astype(jnp.int32).reshape(1)
    query_local = queries[0, 0]
    key_local = key_rows[0, 0]
    value_local = value_rows[0, 0]
    route = []
    for s in range(seq_count):
        for m in range(model_count):
            if m >= KVH:
                route.append((s * model_count + m - KVH, s * model_count + m))
            elif s > 0:
                route.append(((s - 1) * model_count + (blocks - 1) * KVH + m, s * model_count + m))
    halo_keys = lax.ppermute(key_local[row_count - WINDOW :], ("seq", "mp"), route)
    halo_values = lax.ppermute(value_local[row_count - WINDOW :], ("seq", "mp"), route)
    halo_rows = WINDOW
    partial_out, stats, acc = local_part(query_local, key_local, value_local, halo_rows)
    weights, merged = weigh_part(opening, query_local, halo_keys, stats)
    attended = gather_part(opening, weights, halo_values, merged, acc, partial_out)
    return attended.reshape(1, 1, row_count, queries.shape[3])


def solution(mesh):
    in_specs = (P("seq", "mp", None, None), P("seq", "mp", None, None), P("seq", "mp", None, None))
    out_specs = P("seq", "mp", None, None)
    return jax.shard_map(
        per_device, mesh=mesh, in_specs=in_specs, out_specs=out_specs, check_vma=False
    )
```

```python
import jax
import jax.numpy as jnp
from jax import lax
from jax.experimental import pallas as pl
from jax.experimental.pallas import tpu as pltpu
from jax.sharding import PartitionSpec as P

KVH = 8
QPK = 2
WINDOW = 1024
QUERY_TILE = 256
LANES = 128


scale_factor = 168.0 ** (-0.5)


def tile_scores(query_tile, key_tile):
    raw = lax.dot_general(
        query_tile, key_tile, (((1,), (1,)), ((), ())), preferred_element_type=jnp.float32
    )
    return raw * scale_factor


def packed_stats(row_top, row_total):
    lane = lax.broadcasted_iota(jnp.int32, (row_top.shape[0], LANES), 1)
    return jnp.where(lane < LANES // 2, row_top, row_total)


def local_kernel(q_ref, k_ref, v_ref, out_ref, stats_ref, acc_ref):
    row_count = q_ref.shape[0]
    halo_rows = stats_ref.shape[0]
    for first_row in range(0, row_count, QUERY_TILE):
        low_key = max(0, first_row - WINDOW + 1) // LANES * LANES
        high_key = first_row + QUERY_TILE
        scores = tile_scores(q_ref[first_row:high_key, :], k_ref[low_key:high_key, :])
        query_pos = first_row + lax.broadcasted_iota(jnp.int32, scores.shape, 0)
        key_pos = low_key + lax.broadcasted_iota(jnp.int32, scores.shape, 1)
        valid = (key_pos <= query_pos) & (query_pos - key_pos < WINDOW)
        scores = jnp.where(valid, scores, -jnp.inf)
        row_top = jnp.max(scores, axis=1, keepdims=True)
        probable = jnp.exp(scores - row_top)
        row_total = jnp.sum(probable, axis=1, keepdims=True)
        context = jnp.dot(
            probable.astype(jnp.bfloat16),
            v_ref[low_key:high_key, :],
            preferred_element_type=jnp.float32,
        )
        if first_row < halo_rows:
            stats_ref[first_row:high_key, :] = packed_stats(row_top, row_total)
            acc_ref[first_row:high_key, :] = context
        else:
            out_ref[first_row:high_key, :] = (context / row_total).astype(out_ref.dtype)


def read_stats(stats_ref, acc_ref, first_row, rows):
    high_row = first_row + rows
    return (
        stats_ref[first_row:high_row, 0:1],
        stats_ref[first_row:high_row, LANES // 2 : LANES // 2 + 1],
        acc_ref[first_row:high_row, :],
    )


def weigh_kernel(opening_ref, q_ref, key_ref, stats_ref, weight_ref, merged_ref):
    halo_rows = stats_ref.shape[0]
    window = key_ref.shape[0]
    shut = opening_ref[0] != 0
    column = 0
    for first_row in range(0, halo_rows, QUERY_TILE):
        high_row = first_row + QUERY_TILE
        local_top, local_total, _ = read_stats(stats_ref, stats_ref, first_row, QUERY_TILE)
        query_tile = q_ref[first_row:high_row, :]
        near = tile_scores(query_tile, key_ref[first_row:high_row, :])
        above = lax.broadcasted_iota(jnp.int32, near.shape, 1) > lax.broadcasted_iota(
            jnp.int32, near.shape, 0
        )
        parts = [jnp.where(above, near, -jnp.inf)]
        if high_row < window:
            parts.append(tile_scores(query_tile, key_ref[high_row:window, :]))
        row_top = local_top
        for scores in parts:
            row_top = jnp.maximum(row_top, jnp.max(scores, axis=1, keepdims=True))
        rescale = jnp.exp(local_top - row_top)
        row_total = rescale * local_total
        for scores in parts:
            probable = jnp.exp(scores - row_top)
            row_total = row_total + jnp.sum(probable, axis=1, keepdims=True)
            width = scores.shape[1]
            weight_ref[:, column : column + width] = probable.astype(weight_ref.dtype)
            column += width
        rescale = jnp.where(shut, 1.0, rescale)
        row_total = jnp.where(shut, local_total, row_total)
        merged_ref[first_row:high_row, :] = packed_stats(rescale, row_total)


def gather_kernel(opening_ref, weight_ref, low_ref, high_ref, merged_ref, acc_ref, _, out_ref):
    halo_rows = merged_ref.shape[0]
    split = low_ref.shape[0]
    window = split + high_ref.shape[0]
    shut = opening_ref[0] != 0
    column = 0
    for first_row in range(0, halo_rows, QUERY_TILE):
        high_row = first_row + QUERY_TILE
        rescale, row_total, local_context = read_stats(merged_ref, acc_ref, first_row, QUERY_TILE)
        context = 0.0
        if first_row < split:
            width = split - first_row
            context = context + jnp.dot(
                weight_ref[:, column : column + width],
                low_ref[first_row:split, :],
                preferred_element_type=jnp.float32,
            )
            column += width
        start = max(first_row, split) - split
        width = window - split - start
        context = context + jnp.dot(
            weight_ref[:, column : column + width],
            high_ref[start:, :],
            preferred_element_type=jnp.float32,
        )
        column += width
        context = rescale * local_context + jnp.where(shut, 0.0, context)
        out_ref[first_row:high_row, :] = (context / row_total).astype(out_ref.dtype)


def local_part(query_local, key_local, value_local, halo_rows):
    row_count, width = query_local.shape
    head_size = key_local.shape[1]
    heads = width // head_size
    head_block = pl.BlockSpec((row_count, head_size), lambda p: (0, p))
    whole = pl.BlockSpec((row_count, head_size), lambda p: (0, 0))
    stat_block = pl.BlockSpec((None, halo_rows, LANES), lambda p: (p, 0, 0))
    acc_block = pl.BlockSpec((None, halo_rows, head_size), lambda p: (p, 0, 0))
    flops = 4 * heads * row_count * (WINDOW + QUERY_TILE) * head_size
    return pl.pallas_call(
        local_kernel,
        grid=(heads,),
        in_specs=[head_block, whole, whole],
        out_specs=[head_block, stat_block, acc_block],
        out_shape=[
            jax.ShapeDtypeStruct((row_count, width), query_local.dtype),
            jax.ShapeDtypeStruct((heads, halo_rows, LANES), jnp.float32),
            jax.ShapeDtypeStruct((heads, halo_rows, head_size), jnp.float32),
        ],
        cost_estimate=pl.CostEstimate(
            flops=flops,
            transcendentals=heads * row_count * (WINDOW + QUERY_TILE),
            bytes_accessed=4 * row_count * width + 8 * heads * halo_rows * LANES,
        ),
    )(query_local, key_local, value_local)


def packed_width(halo_rows, window):
    return sum(window - first_row for first_row in range(0, halo_rows, QUERY_TILE))


def weigh_part(opening, query_local, halo_keys, stats):
    row_count, width = query_local.shape
    window, head_size = halo_keys.shape
    heads = width // head_size
    halo_rows = stats.shape[1]
    weight_width = packed_width(halo_rows, window)
    column = pl.BlockSpec((row_count, head_size), lambda p, o: (0, p))
    halo_block = pl.BlockSpec((window, head_size), lambda p, o: (0, 0))
    stat_block = pl.BlockSpec((None, halo_rows, LANES), lambda p, o: (p, 0, 0))
    weight_block = pl.BlockSpec((None, QUERY_TILE, weight_width), lambda p, o: (p, 0, 0))
    return pl.pallas_call(
        weigh_kernel,
        grid_spec=pltpu.PrefetchScalarGridSpec(
            num_scalar_prefetch=1,
            grid=(heads,),
            in_specs=[column, halo_block, stat_block],
            out_specs=[weight_block, stat_block],
        ),
        out_shape=[
            jax.ShapeDtypeStruct((heads, QUERY_TILE, weight_width), jnp.bfloat16),
            jax.ShapeDtypeStruct((heads, halo_rows, LANES), jnp.float32),
        ],
        cost_estimate=pl.CostEstimate(
            flops=2 * heads * QUERY_TILE * weight_width * head_size,
            transcendentals=heads * QUERY_TILE * weight_width,
            bytes_accessed=row_count * width * 2 + 2 * heads * QUERY_TILE * weight_width
            + 8 * heads * halo_rows * LANES,
        ),
    )(opening, query_local, halo_keys, stats)


def gather_part(opening, weights, low_values, high_values, merged, acc, partial_out):
    row_count, width = partial_out.shape
    split, head_size = low_values.shape
    heads = width // head_size
    halo_rows = merged.shape[1]
    weight_width = weights.shape[2]
    column = pl.BlockSpec((halo_rows, head_size), lambda p, o: (0, p))
    low_block = pl.BlockSpec((split, head_size), lambda p, o: (0, 0))
    high_block = pl.BlockSpec(high_values.shape, lambda p, o: (0, 0))
    stat_block = pl.BlockSpec((None, halo_rows, LANES), lambda p, o: (p, 0, 0))
    acc_block = pl.BlockSpec((None, halo_rows, head_size), lambda p, o: (p, 0, 0))
    weight_block = pl.BlockSpec((None, QUERY_TILE, weight_width), lambda p, o: (p, 0, 0))
    return pl.pallas_call(
        gather_kernel,
        grid_spec=pltpu.PrefetchScalarGridSpec(
            num_scalar_prefetch=1,
            grid=(heads,),
            in_specs=[
                weight_block,
                low_block,
                high_block,
                stat_block,
                acc_block,
                pl.BlockSpec(memory_space=pl.ANY),
            ],
            out_specs=column,
        ),
        out_shape=jax.ShapeDtypeStruct((row_count, width), partial_out.dtype),
        input_output_aliases={6: 0},
        cost_estimate=pl.CostEstimate(
            flops=2 * heads * QUERY_TILE * weight_width * head_size,
            transcendentals=0,
            bytes_accessed=2 * heads * QUERY_TILE * weight_width + 2 * row_count * width * 2
            + 8 * heads * halo_rows * LANES,
        ),
    )(opening, weights, low_values, high_values, merged, acc, partial_out)


def per_device(queries, key_rows, value_rows):
    row_count = queries.shape[2]
    seq_count = lax.axis_size("seq")
    model_count = lax.axis_size("mp")
    blocks = model_count // KVH
    row_block = lax.axis_index("mp") // KVH
    opening = jnp.logical_and(lax.axis_index("seq") == 0, row_block == 0)
    opening = opening.astype(jnp.int32).reshape(1)
    query_local = queries[0, 0]
    key_local = key_rows[0, 0]
    value_local = value_rows[0, 0]
    route = []
    for s in range(seq_count):
        for m in range(model_count):
            if m >= KVH:
                route.append((s * model_count + m - KVH, s * model_count + m))
            elif s > 0:
                route.append(((s - 1) * model_count + (blocks - 1) * KVH + m, s * model_count + m))
    halo_keys = lax.ppermute(key_local[row_count - WINDOW :], ("seq", "mp"), route)
    split_row = row_count - WINDOW // 2
    high_values = lax.ppermute(value_local[split_row:], ("seq", "mp"), route)
    low_values = lax.ppermute(value_local[row_count - WINDOW : split_row], ("seq", "mp"), route)
    halo_rows = WINDOW
    partial_out, stats, acc = local_part(query_local, key_local, value_local, halo_rows)
    weights, merged = weigh_part(opening, query_local, halo_keys, stats)
    attended = gather_part(opening, weights, low_values, high_values, merged, acc, partial_out)
    return attended.reshape(1, 1, row_count, queries.shape[3])


def solution(mesh):
    in_specs = (P("seq", "mp", None, None), P("seq", "mp", None, None), P("seq", "mp", None, None))
    out_specs = P("seq", "mp", None, None)
    return jax.shard_map(
        per_device, mesh=mesh, in_specs=in_specs, out_specs=out_specs, check_vma=False
    )
```

```python
import jax
import jax.numpy as jnp
from jax import lax
from jax.experimental import pallas as pl
from jax.experimental.pallas import tpu as pltpu
from jax.sharding import PartitionSpec as P

KVH = 8
QPK = 2
WINDOW = 1024
QUERY_TILE = 256
LANES = 128


scale_factor = 168.0 ** (-0.5)


def tile_scores(query_tile, key_tile):
    raw = lax.dot_general(
        query_tile, key_tile, (((1,), (1,)), ((), ())), preferred_element_type=jnp.float32
    )
    return raw * scale_factor


def packed_stats(row_top, row_total):
    lane = lax.broadcasted_iota(jnp.int32, (row_top.shape[0], LANES), 1)
    return jnp.where(lane < LANES // 2, row_top, row_total)


def local_kernel(q_ref, k_ref, v_ref, out_ref, stats_ref, acc_ref):
    row_count = q_ref.shape[0]
    halo_rows = stats_ref.shape[0]
    for first_row in range(0, row_count, QUERY_TILE):
        low_key = max(0, first_row - WINDOW + 1) // LANES * LANES
        high_key = first_row + QUERY_TILE
        scores = tile_scores(q_ref[first_row:high_key, :], k_ref[low_key:high_key, :])
        query_pos = first_row + lax.broadcasted_iota(jnp.int32, scores.shape, 0)
        key_pos = low_key + lax.broadcasted_iota(jnp.int32, scores.shape, 1)
        valid = (key_pos <= query_pos) & (query_pos - key_pos < WINDOW)
        scores = jnp.where(valid, scores, -jnp.inf)
        row_top = jnp.max(scores, axis=1, keepdims=True)
        probable = jnp.exp(scores - row_top)
        row_total = jnp.sum(probable, axis=1, keepdims=True)
        context = jnp.dot(
            probable.astype(jnp.bfloat16),
            v_ref[low_key:high_key, :],
            preferred_element_type=jnp.float32,
        )
        if first_row < halo_rows:
            stats_ref[first_row:high_key, :] = packed_stats(row_top, row_total)
            acc_ref[first_row:high_key, :] = context
        else:
            out_ref[first_row:high_key, :] = (context / row_total).astype(out_ref.dtype)


def read_stats(stats_ref, acc_ref, first_row, rows):
    high_row = first_row + rows
    return (
        stats_ref[first_row:high_row, 0:1],
        stats_ref[first_row:high_row, LANES // 2 : LANES // 2 + 1],
        acc_ref[first_row:high_row, :],
    )


def weigh_kernel(opening_ref, q_ref, key_ref, stats_ref, weight_ref, merged_ref):
    halo_rows = stats_ref.shape[0]
    window = key_ref.shape[0]
    shut = opening_ref[0] != 0
    column = 0
    for first_row in range(0, halo_rows, QUERY_TILE):
        high_row = first_row + QUERY_TILE
        local_top, local_total, _ = read_stats(stats_ref, stats_ref, first_row, QUERY_TILE)
        query_tile = q_ref[first_row:high_row, :]
        near = tile_scores(query_tile, key_ref[first_row:high_row, :])
        above = lax.broadcasted_iota(jnp.int32, near.shape, 1) > lax.broadcasted_iota(
            jnp.int32, near.shape, 0
        )
        parts = [jnp.where(above, near, -jnp.inf)]
        if high_row < window:
            parts.append(tile_scores(query_tile, key_ref[high_row:window, :]))
        row_top = local_top
        for scores in parts:
            row_top = jnp.maximum(row_top, jnp.max(scores, axis=1, keepdims=True))
        rescale = jnp.exp(local_top - row_top)
        row_total = rescale * local_total
        for scores in parts:
            probable = jnp.exp(scores - row_top)
            row_total = row_total + jnp.sum(probable, axis=1, keepdims=True)
            width = scores.shape[1]
            weight_ref[:, column : column + width] = probable.astype(weight_ref.dtype)
            column += width
        rescale = jnp.where(shut, 1.0, rescale)
        row_total = jnp.where(shut, local_total, row_total)
        merged_ref[first_row:high_row, :] = packed_stats(rescale, row_total)


def gather_kernel(opening_ref, weight_ref, *refs):
    piece_refs = refs[:-4]
    merged_ref, acc_ref, _, out_ref = refs[-4:]
    halo_rows = merged_ref.shape[0]
    shut = opening_ref[0] != 0
    bounds = [0]
    for piece_ref in piece_refs:
        bounds.append(bounds[-1] + piece_ref.shape[0])
    column = 0
    for first_row in range(0, halo_rows, QUERY_TILE):
        high_row = first_row + QUERY_TILE
        rescale, row_total, local_context = read_stats(merged_ref, acc_ref, first_row, QUERY_TILE)
        context = 0.0
        for index, piece_ref in enumerate(piece_refs):
            low, high = bounds[index], bounds[index + 1]
            start = max(low, first_row)
            if start >= high:
                continue
            width = high - start
            context = context + jnp.dot(
                weight_ref[:, column : column + width],
                piece_ref[start - low :, :],
                preferred_element_type=jnp.float32,
            )
            column += width
        context = rescale * local_context + jnp.where(shut, 0.0, context)
        out_ref[first_row:high_row, :] = (context / row_total).astype(out_ref.dtype)


def local_part(query_local, key_local, value_local, halo_rows):
    row_count, width = query_local.shape
    head_size = key_local.shape[1]
    heads = width // head_size
    head_block = pl.BlockSpec((row_count, head_size), lambda p: (0, p))
    whole = pl.BlockSpec((row_count, head_size), lambda p: (0, 0))
    stat_block = pl.BlockSpec((None, halo_rows, LANES), lambda p: (p, 0, 0))
    acc_block = pl.BlockSpec((None, halo_rows, head_size), lambda p: (p, 0, 0))
    flops = 4 * heads * row_count * (WINDOW + QUERY_TILE) * head_size
    return pl.pallas_call(
        local_kernel,
        grid=(heads,),
        in_specs=[head_block, whole, whole],
        out_specs=[head_block, stat_block, acc_block],
        out_shape=[
            jax.ShapeDtypeStruct((row_count, width), query_local.dtype),
            jax.ShapeDtypeStruct((heads, halo_rows, LANES), jnp.float32),
            jax.ShapeDtypeStruct((heads, halo_rows, head_size), jnp.float32),
        ],
        cost_estimate=pl.CostEstimate(
            flops=flops,
            transcendentals=heads * row_count * (WINDOW + QUERY_TILE),
            bytes_accessed=4 * row_count * width + 8 * heads * halo_rows * LANES,
        ),
    )(query_local, key_local, value_local)


def packed_width(halo_rows, window):
    return sum(window - first_row for first_row in range(0, halo_rows, QUERY_TILE))


def weigh_part(opening, query_local, halo_keys, stats):
    row_count, width = query_local.shape
    window, head_size = halo_keys.shape
    heads = width // head_size
    halo_rows = stats.shape[1]
    weight_width = packed_width(halo_rows, window)
    column = pl.BlockSpec((row_count, head_size), lambda p, o: (0, p))
    halo_block = pl.BlockSpec((window, head_size), lambda p, o: (0, 0))
    stat_block = pl.BlockSpec((None, halo_rows, LANES), lambda p, o: (p, 0, 0))
    weight_block = pl.BlockSpec((None, QUERY_TILE, weight_width), lambda p, o: (p, 0, 0))
    return pl.pallas_call(
        weigh_kernel,
        grid_spec=pltpu.PrefetchScalarGridSpec(
            num_scalar_prefetch=1,
            grid=(heads,),
            in_specs=[column, halo_block, stat_block],
            out_specs=[weight_block, stat_block],
        ),
        out_shape=[
            jax.ShapeDtypeStruct((heads, QUERY_TILE, weight_width), jnp.bfloat16),
            jax.ShapeDtypeStruct((heads, halo_rows, LANES), jnp.float32),
        ],
        cost_estimate=pl.CostEstimate(
            flops=2 * heads * QUERY_TILE * weight_width * head_size,
            transcendentals=heads * QUERY_TILE * weight_width,
            bytes_accessed=row_count * width * 2 + 2 * heads * QUERY_TILE * weight_width
            + 8 * heads * halo_rows * LANES,
        ),
    )(opening, query_local, halo_keys, stats)


def gather_part(opening, weights, pieces, merged, acc, partial_out):
    row_count, width = partial_out.shape
    head_size = pieces[0].shape[1]
    heads = width // head_size
    halo_rows = merged.shape[1]
    weight_width = weights.shape[2]
    column = pl.BlockSpec((halo_rows, head_size), lambda p, o: (0, p))
    piece_blocks = [pl.BlockSpec(piece.shape, lambda p, o: (0, 0)) for piece in pieces]
    stat_block = pl.BlockSpec((None, halo_rows, LANES), lambda p, o: (p, 0, 0))
    acc_block = pl.BlockSpec((None, halo_rows, head_size), lambda p, o: (p, 0, 0))
    weight_block = pl.BlockSpec((None, QUERY_TILE, weight_width), lambda p, o: (p, 0, 0))
    return pl.pallas_call(
        gather_kernel,
        grid_spec=pltpu.PrefetchScalarGridSpec(
            num_scalar_prefetch=1,
            grid=(heads,),
            in_specs=[weight_block, *piece_blocks, stat_block, acc_block,
                      pl.BlockSpec(memory_space=pl.ANY)],
            out_specs=column,
        ),
        out_shape=jax.ShapeDtypeStruct((row_count, width), partial_out.dtype),
        input_output_aliases={4 + len(pieces): 0},
        cost_estimate=pl.CostEstimate(
            flops=2 * heads * QUERY_TILE * weight_width * head_size,
            transcendentals=0,
            bytes_accessed=2 * heads * QUERY_TILE * weight_width + 2 * row_count * width * 2
            + 8 * heads * halo_rows * LANES,
        ),
    )(opening, weights, *pieces, merged, acc, partial_out)


def per_device(queries, key_rows, value_rows):
    row_count = queries.shape[2]
    seq_count = lax.axis_size("seq")
    model_count = lax.axis_size("mp")
    blocks = model_count // KVH
    row_block = lax.axis_index("mp") // KVH
    opening = jnp.logical_and(lax.axis_index("seq") == 0, row_block == 0)
    opening = opening.astype(jnp.int32).reshape(1)
    query_local = queries[0, 0]
    key_local = key_rows[0, 0]
    value_local = value_rows[0, 0]
    route = []
    for s in range(seq_count):
        for m in range(model_count):
            if m >= KVH:
                route.append((s * model_count + m - KVH, s * model_count + m))
            elif s > 0:
                route.append(((s - 1) * model_count + (blocks - 1) * KVH + m, s * model_count + m))
    halo_keys = lax.ppermute(key_local[row_count - WINDOW :], ("seq", "mp"), route)
    first = row_count - WINDOW
    cuts = [first, first + 384, first + 640, row_count]
    pieces = [
        lax.ppermute(value_local[cuts[i] : cuts[i + 1]], ("seq", "mp"), route)
        for i in (2, 1, 0)
    ][::-1]
    halo_rows = WINDOW
    partial_out, stats, acc = local_part(query_local, key_local, value_local, halo_rows)
    weights, merged = weigh_part(opening, query_local, halo_keys, stats)
    attended = gather_part(opening, weights, pieces, merged, acc, partial_out)
    return attended.reshape(1, 1, row_count, queries.shape[3])


def solution(mesh):
    in_specs = (P("seq", "mp", None, None), P("seq", "mp", None, None), P("seq", "mp", None, None))
    out_specs = P("seq", "mp", None, None)
    return jax.shard_map(
        per_device, mesh=mesh, in_specs=in_specs, out_specs=out_specs, check_vma=False
    )
```

```python
import jax
import jax.numpy as jnp
from jax import lax
from jax.experimental import pallas as pl
from jax.experimental.pallas import tpu as pltpu
from jax.sharding import PartitionSpec as P

KVH = 8
QPK = 2
WINDOW = 1024
QUERY_TILE = 256
LANES = 128


scale_factor = 168.0 ** (-0.5)


def tile_scores(query_tile, key_tile):
    raw = lax.dot_general(
        query_tile, key_tile, (((1,), (1,)), ((), ())), preferred_element_type=jnp.float32
    )
    return raw * scale_factor


def packed_stats(row_top, row_total):
    lane = lax.broadcasted_iota(jnp.int32, (row_top.shape[0], LANES), 1)
    return jnp.where(lane < LANES // 2, row_top, row_total)


def local_kernel(q_ref, k_ref, v_ref, out_ref, stats_ref, acc_ref):
    row_count = q_ref.shape[0]
    halo_rows = stats_ref.shape[0]
    for first_row in range(0, row_count, QUERY_TILE):
        low_key = max(0, first_row - WINDOW + 1) // LANES * LANES
        high_key = first_row + QUERY_TILE
        scores = tile_scores(q_ref[first_row:high_key, :], k_ref[low_key:high_key, :])
        query_pos = first_row + lax.broadcasted_iota(jnp.int32, scores.shape, 0)
        key_pos = low_key + lax.broadcasted_iota(jnp.int32, scores.shape, 1)
        valid = (key_pos <= query_pos) & (query_pos - key_pos < WINDOW)
        scores = jnp.where(valid, scores, -jnp.inf)
        row_top = jnp.max(scores, axis=1, keepdims=True)
        probable = jnp.exp(scores - row_top)
        row_total = jnp.sum(probable, axis=1, keepdims=True)
        context = jnp.dot(
            probable.astype(jnp.bfloat16),
            v_ref[low_key:high_key, :],
            preferred_element_type=jnp.float32,
        )
        if first_row < halo_rows:
            stats_ref[first_row:high_key, :] = packed_stats(row_top, row_total)
            acc_ref[first_row:high_key, :] = context
        else:
            out_ref[first_row:high_key, :] = (context / row_total).astype(out_ref.dtype)


def read_stats(stats_ref, acc_ref, first_row, rows):
    high_row = first_row + rows
    return (
        stats_ref[first_row:high_row, 0:1],
        stats_ref[first_row:high_row, LANES // 2 : LANES // 2 + 1],
        acc_ref[first_row:high_row, :],
    )


def weigh_kernel(opening_ref, q_ref, key_ref, stats_ref, weight_ref, merged_ref):
    halo_rows = stats_ref.shape[0]
    window = key_ref.shape[0]
    shut = opening_ref[0] != 0
    column = 0
    for first_row in range(0, halo_rows, QUERY_TILE):
        high_row = first_row + QUERY_TILE
        local_top, local_total, _ = read_stats(stats_ref, stats_ref, first_row, QUERY_TILE)
        query_tile = q_ref[first_row:high_row, :]
        near = tile_scores(query_tile, key_ref[first_row:high_row, :])
        above = lax.broadcasted_iota(jnp.int32, near.shape, 1) > lax.broadcasted_iota(
            jnp.int32, near.shape, 0
        )
        parts = [jnp.where(above, near, -jnp.inf)]
        if high_row < window:
            parts.append(tile_scores(query_tile, key_ref[high_row:window, :]))
        row_top = local_top
        for scores in parts:
            row_top = jnp.maximum(row_top, jnp.max(scores, axis=1, keepdims=True))
        rescale = jnp.exp(local_top - row_top)
        row_total = rescale * local_total
        for scores in parts:
            probable = jnp.exp(scores - row_top)
            row_total = row_total + jnp.sum(probable, axis=1, keepdims=True)
            width = scores.shape[1]
            weight_ref[:, column : column + width] = jnp.where(shut, 0.0, probable).astype(
                weight_ref.dtype
            )
            column += width
        rescale = jnp.where(shut, 1.0, rescale)
        row_total = jnp.where(shut, local_total, row_total)
        merged_ref[first_row:high_row, :] = packed_stats(rescale, row_total)


def gather_kernel(weight_ref, low_ref, high_ref, merged_ref, acc_ref, _, out_ref):
    halo_rows = merged_ref.shape[0]
    split = low_ref.shape[0]
    window = split + high_ref.shape[0]
    column = 0
    for first_row in range(0, halo_rows, QUERY_TILE):
        high_row = first_row + QUERY_TILE
        rescale, row_total, local_context = read_stats(merged_ref, acc_ref, first_row, QUERY_TILE)
        context = 0.0
        if first_row < split:
            width = split - first_row
            context = context + jnp.dot(
                weight_ref[:, column : column + width],
                low_ref[first_row:split, :],
                preferred_element_type=jnp.float32,
            )
            column += width
        start = max(first_row, split) - split
        width = window - split - start
        context = context + jnp.dot(
            weight_ref[:, column : column + width],
            high_ref[start:, :],
            preferred_element_type=jnp.float32,
        )
        column += width
        context = rescale * local_context + context
        out_ref[first_row:high_row, :] = (context / row_total).astype(out_ref.dtype)


def local_part(query_local, key_local, value_local, halo_rows):
    row_count, width = query_local.shape
    head_size = key_local.shape[1]
    heads = width // head_size
    head_block = pl.BlockSpec((row_count, head_size), lambda p: (0, p))
    whole = pl.BlockSpec((row_count, head_size), lambda p: (0, 0))
    stat_block = pl.BlockSpec((None, halo_rows, LANES), lambda p: (p, 0, 0))
    acc_block = pl.BlockSpec((None, halo_rows, head_size), lambda p: (p, 0, 0))
    flops = 4 * heads * row_count * (WINDOW + QUERY_TILE) * head_size
    return pl.pallas_call(
        local_kernel,
        grid=(heads,),
        in_specs=[head_block, whole, whole],
        out_specs=[head_block, stat_block, acc_block],
        out_shape=[
            jax.ShapeDtypeStruct((row_count, width), query_local.dtype),
            jax.ShapeDtypeStruct((heads, halo_rows, LANES), jnp.float32),
            jax.ShapeDtypeStruct((heads, halo_rows, head_size), jnp.float32),
        ],
        cost_estimate=pl.CostEstimate(
            flops=flops,
            transcendentals=heads * row_count * (WINDOW + QUERY_TILE),
            bytes_accessed=4 * row_count * width + 8 * heads * halo_rows * LANES,
        ),
    )(query_local, key_local, value_local)


def packed_width(halo_rows, window):
    return sum(window - first_row for first_row in range(0, halo_rows, QUERY_TILE))


def weigh_part(opening, query_local, halo_keys, stats):
    row_count, width = query_local.shape
    window, head_size = halo_keys.shape
    heads = width // head_size
    halo_rows = stats.shape[1]
    weight_width = packed_width(halo_rows, window)
    column = pl.BlockSpec((row_count, head_size), lambda p, o: (0, p))
    halo_block = pl.BlockSpec((window, head_size), lambda p, o: (0, 0))
    stat_block = pl.BlockSpec((None, halo_rows, LANES), lambda p, o: (p, 0, 0))
    weight_block = pl.BlockSpec((None, QUERY_TILE, weight_width), lambda p, o: (p, 0, 0))
    return pl.pallas_call(
        weigh_kernel,
        grid_spec=pltpu.PrefetchScalarGridSpec(
            num_scalar_prefetch=1,
            grid=(heads,),
            in_specs=[column, halo_block, stat_block],
            out_specs=[weight_block, stat_block],
        ),
        out_shape=[
            jax.ShapeDtypeStruct((heads, QUERY_TILE, weight_width), jnp.bfloat16),
            jax.ShapeDtypeStruct((heads, halo_rows, LANES), jnp.float32),
        ],
        cost_estimate=pl.CostEstimate(
            flops=2 * heads * QUERY_TILE * weight_width * head_size,
            transcendentals=heads * QUERY_TILE * weight_width,
            bytes_accessed=row_count * width * 2 + 2 * heads * QUERY_TILE * weight_width
            + 8 * heads * halo_rows * LANES,
        ),
    )(opening, query_local, halo_keys, stats)


def gather_part(weights, low_values, high_values, merged, acc, partial_out):
    row_count, width = partial_out.shape
    split, head_size = low_values.shape
    heads = width // head_size
    halo_rows = merged.shape[1]
    weight_width = weights.shape[2]
    column = pl.BlockSpec((halo_rows, head_size), lambda p: (0, p))
    low_block = pl.BlockSpec((split, head_size), lambda p: (0, 0))
    high_block = pl.BlockSpec(high_values.shape, lambda p: (0, 0))
    stat_block = pl.BlockSpec((None, halo_rows, LANES), lambda p: (p, 0, 0))
    acc_block = pl.BlockSpec((None, halo_rows, head_size), lambda p: (p, 0, 0))
    weight_block = pl.BlockSpec((None, QUERY_TILE, weight_width), lambda p: (p, 0, 0))
    return pl.pallas_call(
        gather_kernel,
        grid_spec=pl.GridSpec(
            grid=(heads,),
            in_specs=[
                weight_block,
                low_block,
                high_block,
                stat_block,
                acc_block,
                pl.BlockSpec(memory_space=pl.ANY),
            ],
            out_specs=column,
        ),
        out_shape=jax.ShapeDtypeStruct((row_count, width), partial_out.dtype),
        input_output_aliases={5: 0},
        cost_estimate=pl.CostEstimate(
            flops=2 * heads * QUERY_TILE * weight_width * head_size,
            transcendentals=0,
            bytes_accessed=2 * heads * QUERY_TILE * weight_width + 2 * row_count * width * 2
            + 8 * heads * halo_rows * LANES,
        ),
    )(weights, low_values, high_values, merged, acc, partial_out)


def per_device(queries, key_rows, value_rows):
    row_count = queries.shape[2]
    seq_count = lax.axis_size("seq")
    model_count = lax.axis_size("mp")
    blocks = model_count // KVH
    row_block = lax.axis_index("mp") // KVH
    opening = jnp.logical_and(lax.axis_index("seq") == 0, row_block == 0)
    opening = opening.astype(jnp.int32).reshape(1)
    query_local = queries[0, 0]
    key_local = key_rows[0, 0]
    value_local = value_rows[0, 0]
    route = []
    for s in range(seq_count):
        for m in range(model_count):
            if m >= KVH:
                route.append((s * model_count + m - KVH, s * model_count + m))
            elif s > 0:
                route.append(((s - 1) * model_count + (blocks - 1) * KVH + m, s * model_count + m))
    halo_keys = lax.ppermute(key_local[row_count - WINDOW :], ("seq", "mp"), route)
    split_row = row_count - WINDOW // 2
    high_values = lax.ppermute(value_local[split_row:], ("seq", "mp"), route)
    low_values = lax.ppermute(value_local[row_count - WINDOW : split_row], ("seq", "mp"), route)
    halo_rows = WINDOW
    partial_out, stats, acc = local_part(query_local, key_local, value_local, halo_rows)
    weights, merged = weigh_part(opening, query_local, halo_keys, stats)
    attended = gather_part(weights, low_values, high_values, merged, acc, partial_out)
    return attended.reshape(1, 1, row_count, queries.shape[3])


def solution(mesh):
    in_specs = (P("seq", "mp", None, None), P("seq", "mp", None, None), P("seq", "mp", None, None))
    out_specs = P("seq", "mp", None, None)
    return jax.shard_map(
        per_device, mesh=mesh, in_specs=in_specs, out_specs=out_specs, check_vma=False
    )
```
